256 devices in a mesh: dp: 4 (over x), ctx: 16 (over z, core), mp: 4 (over y).
Axes of the slice: x: 4, y: 4, z: 8, core: 2. Of those that a mesh axis runs over, the one named last changes fastest.
Arguments:
- queries: bfloat16 [65536, 2048], P(('dp', 'ctx'), 'mp'), parts along dimension 0, may hold values from -6 to 6
- keys: bfloat16 [65536, 2048], P(('dp', 'ctx'), 'mp'), parts along dimension 0, may hold values from -6 to 6
- values: bfloat16 [65536, 2048], P(('dp', 'ctx'), 'mp'), parts along dimension 0, may hold values from -6 to 6
- segment_ids: int32 [65536], P(('dp', 'ctx')), parts along dimension 0, may hold values from 0 to 5, never falling along the last dimension, each value on 1 to 8192 neighbouring positions
- norm_gain: float32 [2048], P('mp'), may hold values from 0.5 to 1.5
- out_weight: bfloat16 [2048, 4096], P(None, 'mp'), may hold values from -0.125 to 0.125
Outputs:
- projected: bfloat16 [65536, 4096], P(('dp', 'ctx'), 'mp'), parts along dimension 0
The draws below stay inside these ranges and needn't reach their ends.
There are 4 independent parts, one for each index of `dp`. The reference program is written for one: setup_inputs(seed, part) draws one part's arguments, and reference() takes and returns one part's arrays. A program takes and returns all parts, laid end to end along the dimension named above; an argument that names none is the same for every part. Nothing has to cross between parts.
Inputs may be any that keep to these rules, and one draw needn't show every extreme that they name: `segment_ids`: ids never fall along the stream; 6 segments, each of 1 to 8192 consecutive positions, one of exactly 8192.
All inputs are finite; a program needn't handle non-finite values.
Results may differ from the reference program's by a relative error of at most 0.0053.
Values may be sent and summed in bfloat16 or wider, within the bound.
No kernel may reach another device: no remote copies, remote signals or barrier semaphores. Data moves between devices by JAX's collectives and lax.ppermute only.
A program may use at most 64 MiB of HBM per device.

```python
import math
import jax
import jax.numpy as jnp
import numpy as np
from jax import lax

D = 4096
HEAD = 128
H = 16
TOK_DEV = 1024
SEGS = 6
HD = 2048
LENGTH = 16384
SEG_MOST = 8192
N_CTX = 16


def block_scale(rng, extent, shards, least, high):
    level, own = 1.0, jax.random.fold_in(rng, 6)
    for dim, shards_of in shards:
        steps = jnp.exp(jax.random.uniform(jax.random.fold_in(own, dim), (shards_of,), jnp.float32, least / len(shards), high / len(shards)))
        level = level * jnp.repeat(steps, extent[dim] // shards_of).reshape([-1 if axis == dim else 1 for axis in range(len(extent))])
    return level


def length_profile(amount, total, reach, slope):
    loads = [(1 << 20) // math.isqrt(standing ** slope) + 1 for standing in range(2, amount + 1)]
    surplus, given = total - reach - (amount - 1), [1] * (amount - 1)
    while surplus > 0:
        candidates = [i for i in range(amount - 1) if given[i] < reach]
        pool, remaining = sum([loads[i] for i in candidates]), surplus
        for i in candidates:
            extra = min(reach - given[i], max(1, remaining * loads[i] // pool), surplus)
            given[i] = given[i] + extra
            surplus = surplus - extra
    return np.array([reach] + given)


def uneven(rng, amount, total, bound, slope):
    if amount == 2:
        one = jax.random.randint(rng, (), max(1, total - bound), min(bound, total - 1) + 1)
        return jnp.stack([one, total - one])
    tallies = jnp.asarray(length_profile(amount, total, bound, slope), jnp.int32)
    couples = (amount - 1) // 2
    source_of, taker = tallies[1:1 + 2 * couples:2], tallies[2:2 + 2 * couples:2]
    room = jnp.minimum(source_of - 1, bound - taker)
    passed = jax.random.randint(jax.random.fold_in(rng, 1), (couples,), 0, 1 << 20) % (room + 1)
    tallies = tallies.at[1:1 + 2 * couples:2].set(source_of - passed).at[2:2 + 2 * couples:2].set(taker + passed)
    return tallies[jax.random.permutation(jax.random.fold_in(rng, 2), amount)]


def centred(key, extent, width, most, split=(), kind=jnp.bfloat16):
    result = jax.random.normal(key, extent, jnp.float32) * width
    if len(split) > 0:
        result = block_scale(key, extent, split, -0.22, 0.18) * result
    return jnp.clip(result, min=-most, max=most).astype(kind)


def setup_inputs(seed: int = 0, part: int = 0) -> dict:
    seeds = jax.random.split(jax.random.key(seed), 7)
    own_keys = jax.random.split(jax.random.fold_in(seeds[6], part), 7)
    return {
        "queries": centred(own_keys[0], (LENGTH, HD), 1.0, 6.0, ((0, 16), (1, 4))),
        "keys": centred(own_keys[1], (LENGTH, HD), 1.0, 6.0, ((0, 16), (1, 4))),
        "values": centred(own_keys[2], (LENGTH, HD), 1.0, 6.0, ((0, 16), (1, 4))),
        "segment_ids": jnp.searchsorted(jnp.cumsum(uneven(own_keys[3], SEGS, LENGTH, SEG_MOST, 1)), jnp.arange(LENGTH), side="right").astype(jnp.int32),
        "norm_gain": jnp.clip(1.0 + 0.1 * jax.random.normal(seeds[4], (HD,), jnp.float32), 0.5, 1.5),
        "out_weight": centred(seeds[5], (HD, D), HD ** -0.5, 0.125, ((1, 4),)),
    }


def features(raw_input):
    return (jax.nn.elu(raw_input.astype(jnp.float32)) + 1.0).astype(jnp.bfloat16)

def reference(queries, keys, values, segment_ids, norm_gain, out_weight):
    feat_query = features(queries).reshape(N_CTX, TOK_DEV, H, HEAD)
    feat_key = features(keys).reshape(N_CTX, TOK_DEV, H, HEAD)
    value_heads = values.reshape(N_CTX, TOK_DEV, H, HEAD)
    segment = segment_ids.reshape(N_CTX, TOK_DEV)
    position = jnp.arange(TOK_DEV)
    causal = position[None, :] <= position[:, None]
    gain_heads = norm_gain.astype(jnp.float32).reshape(H, HEAD)

    def one_block(carry, pieces):
        state_sum, final_seg = carry
        block_query, block_key, block_value, block_seg = pieces
        carry_on = (block_seg == final_seg).astype(jnp.float32)
        allowed = causal & (block_seg[:, None] == block_seg[None, :])
        scores = jnp.einsum('thd,shd->hts', block_query.astype(jnp.float32), block_key.astype(jnp.float32))
        weights = jnp.where(allowed[None], scores, 0.0).astype(jnp.bfloat16)
        inside = jnp.einsum('hts,she->the', weights.astype(jnp.float32), block_value.astype(jnp.float32))
        state_hi = state_sum.astype(jnp.bfloat16)
        state_lo = (state_sum - state_hi.astype(jnp.float32)).astype(jnp.bfloat16)
        query_wide = block_query.astype(jnp.float32)
        carried = jnp.einsum('thd,hde->the', query_wide, state_hi.astype(jnp.float32)) + jnp.einsum('thd,hde->the', query_wide, state_lo.astype(jnp.float32))
        numerator = inside + carry_on[:, None, None] * carried
        normed = numerator * lax.rsqrt(lax.optimization_barrier(jnp.mean(numerator * numerator, axis=-1, keepdims=True)) + 1e-06)
        hidden = (normed * gain_heads[None]).astype(jnp.bfloat16).reshape(TOK_DEV, HD)
        block_last = block_seg[-1]
        in_final = (block_seg == block_last).astype(jnp.float32)
        local_sum = jnp.einsum('thd,the->hde', block_key.astype(jnp.float32) * in_final[:, None, None], block_value.astype(jnp.float32))
        state_sum = local_sum + jnp.where(block_last == final_seg, state_sum, 0.0)
        return ((state_sum, block_last), hidden)
    initial = (jnp.zeros((H, HEAD, HEAD), jnp.float32), jnp.int32(-1))
    _, hidden_all = lax.scan(one_block, initial, (feat_query, feat_key, value_heads, segment))
    hidden_all = hidden_all.reshape(LENGTH, HD)
    return jnp.dot(hidden_all, out_weight, preferred_element_type=jnp.float32).astype(jnp.bfloat16)
```

```python
import jax
import jax.numpy as jnp
from jax import lax
from jax.sharding import PartitionSpec as P

HEAD = 128


def features(raw_input):
    return (jax.nn.elu(raw_input.astype(jnp.float32)) + 1.0).astype(jnp.bfloat16)


def carried_in(local_sum, final_seg, axis):
    count = lax.axis_size(axis)
    shape = local_sum.shape
    flat = local_sum.reshape(count, -1)
    width = flat.shape[1]
    seg_row = jnp.full((count, HEAD), final_seg.astype(jnp.float32))
    sent = jnp.concatenate([flat, seg_row], axis=1)
    pieces = lax.all_to_all(sent, axis, 0, 0, tiled=True)
    sums = pieces[:, :width]
    segs = pieces[:, width]
    block = jnp.arange(count)
    prev_seg = jnp.concatenate([jnp.full((1,), -1.0, jnp.float32), segs[:-1]])
    mask = (block[None, :] < block[:, None]) & (segs[None, :] == prev_seg[:, None])
    carry = jnp.sum(jnp.where(mask[:, :, None], sums[None, :, :], 0.0), axis=1)
    back = jnp.concatenate([carry, jnp.broadcast_to(prev_seg[:, None], (count, HEAD))], axis=1)
    mine = lax.all_to_all(back, axis, 0, 0, tiled=True)
    before_sum = mine[:, :width].reshape(shape)
    before_seg = mine[0, width]
    return before_sum, before_seg


def per_device(queries, keys, values, segment_ids, norm_gain, out_weight):
    rows_here = queries.shape[0]
    width_here = queries.shape[1]
    heads_here = width_here // HEAD
    feat_query = features(queries).reshape(rows_here, heads_here, HEAD)
    feat_key = features(keys).reshape(rows_here, heads_here, HEAD)
    value_heads = values.reshape(rows_here, heads_here, HEAD)
    final_seg = segment_ids[rows_here - 1]
    in_final = (segment_ids == final_seg).astype(jnp.bfloat16)
    local_sum = jnp.einsum(
        "thd,the->hde",
        feat_key * in_final[:, None, None],
        value_heads,
        preferred_element_type=jnp.float32,
    )
    before_sum, before_seg = carried_in(local_sum, final_seg, "ctx")
    position = jnp.arange(rows_here)
    allowed = (position[None, :] <= position[:, None]) & (
        segment_ids[:, None] == segment_ids[None, :]
    )
    scores = jnp.einsum("thd,shd->hts", feat_query, feat_key, preferred_element_type=jnp.float32)
    weights = jnp.where(allowed[None], scores, 0.0).astype(jnp.bfloat16)
    inside = jnp.einsum("hts,she->the", weights, value_heads, preferred_element_type=jnp.float32)
    state_hi = before_sum.astype(jnp.bfloat16)
    state_lo = (before_sum - state_hi.astype(jnp.float32)).astype(jnp.bfloat16)
    carried = jnp.einsum(
        "thd,hde->the", feat_query, state_hi, preferred_element_type=jnp.float32
    ) + jnp.einsum("thd,hde->the", feat_query, state_lo, preferred_element_type=jnp.float32)
    carry_on = (segment_ids.astype(jnp.float32) == before_seg).astype(jnp.float32)
    numerator = inside + carry_on[:, None, None] * carried
    normed = numerator * lax.rsqrt(jnp.mean(numerator * numerator, axis=-1, keepdims=True) + 1e-06)
    gain_heads = norm_gain.reshape(heads_here, HEAD)
    hidden = (normed * gain_heads[None]).astype(jnp.bfloat16).reshape(rows_here, width_here)
    projected = jnp.dot(
        lax.all_gather(hidden, "mp", axis=1, tiled=True),
        out_weight,
        preferred_element_type=jnp.float32,
    )
    return projected.astype(jnp.bfloat16)


def solution(mesh):
    in_specs = (
        P(("dp", "ctx"), "mp"),
        P(("dp", "ctx"), "mp"),
        P(("dp", "ctx"), "mp"),
        P(("dp", "ctx")),
        P("mp"),
        P(None, "mp"),
    )
    out_specs = P(("dp", "ctx"), "mp")
    return jax.shard_map(
        per_device, mesh=mesh, in_specs=in_specs, out_specs=out_specs, check_vma=False
    )
```

```python
import jax
import jax.numpy as jnp
from jax import lax
from jax.sharding import PartitionSpec as P

HEAD = 128


def features(raw_input):
    return (jax.nn.elu(raw_input.astype(jnp.float32)) + 1.0).astype(jnp.bfloat16)


def carried_in(local_sum, final_seg, axis):
    count = lax.axis_size(axis)
    shape = local_sum.shape
    flat = local_sum.reshape(count, -1)
    width = flat.shape[1]
    seg_row = jnp.full((count, HEAD), final_seg.astype(jnp.float32))
    sent = jnp.concatenate([flat, seg_row], axis=1)
    pieces = lax.all_to_all(sent, axis, 0, 0, tiled=True)
    sums = pieces[:, :width]
    segs = pieces[:, width]
    block = jnp.arange(count)
    prev_seg = jnp.concatenate([jnp.full((1,), -1.0, jnp.float32), segs[:-1]])
    mask = (block[None, :] < block[:, None]) & (segs[None, :] == prev_seg[:, None])
    carry = jnp.sum(jnp.where(mask[:, :, None], sums[None, :, :], 0.0), axis=1)
    back = jnp.concatenate([carry, jnp.broadcast_to(prev_seg[:, None], (count, HEAD))], axis=1)
    mine = lax.all_to_all(back, axis, 0, 0, tiled=True)
    before_sum = mine[:, :width].reshape(shape)
    before_seg = mine[0, width]
    return before_sum, before_seg


def project_gathered(hidden, out_weight, axis):
    count, mine = lax.axis_size(axis), lax.axis_index(axis)
    rows, width = hidden.shape
    half = rows // 2
    weight_groups = out_weight.reshape(count, width, out_weight.shape[1])
    ahead = [(j, (j + 1) % count) for j in range(count)]
    behind = [(j, (j - 1) % count) for j in range(count)]

    def part(block, offset):
        group = lax.rem(mine + offset + count, count)
        return jnp.dot(block, weight_groups[group], preferred_element_type=jnp.float32)

    from_left = lax.ppermute(hidden, axis, ahead)
    from_right = lax.ppermute(hidden, axis, behind)
    far_top = lax.ppermute(from_left[:half], axis, ahead)
    far_bottom = lax.ppermute(from_right[half:], axis, behind)
    total = part(hidden, 0) + part(from_left, -1) + part(from_right, 1)
    far = jnp.concatenate([part(far_top, 2), part(far_bottom, 2)], axis=0)
    return total + far


def per_device(queries, keys, values, segment_ids, norm_gain, out_weight):
    rows_here = queries.shape[0]
    width_here = queries.shape[1]
    heads_here = width_here // HEAD
    feat_query = features(queries).reshape(rows_here, heads_here, HEAD)
    feat_key = features(keys).reshape(rows_here, heads_here, HEAD)
    value_heads = values.reshape(rows_here, heads_here, HEAD)
    final_seg = segment_ids[rows_here - 1]
    in_final = (segment_ids == final_seg).astype(jnp.bfloat16)
    local_sum = jnp.einsum(
        "thd,the->hde",
        feat_key * in_final[:, None, None],
        value_heads,
        preferred_element_type=jnp.float32,
    )
    before_sum, before_seg = carried_in(local_sum, final_seg, "ctx")
    position = jnp.arange(rows_here)
    allowed = (position[None, :] <= position[:, None]) & (
        segment_ids[:, None] == segment_ids[None, :]
    )
    scores = jnp.einsum("thd,shd->hts", feat_query, feat_key, preferred_element_type=jnp.float32)
    weights = jnp.where(allowed[None], scores, 0.0).astype(jnp.bfloat16)
    inside = jnp.einsum("hts,she->the", weights, value_heads, preferred_element_type=jnp.float32)
    state_hi = before_sum.astype(jnp.bfloat16)
    state_lo = (before_sum - state_hi.astype(jnp.float32)).astype(jnp.bfloat16)
    carried = jnp.einsum(
        "thd,hde->the", feat_query, state_hi, preferred_element_type=jnp.float32
    ) + jnp.einsum("thd,hde->the", feat_query, state_lo, preferred_element_type=jnp.float32)
    carry_on = (segment_ids.astype(jnp.float32) == before_seg).astype(jnp.float32)
    numerator = inside + carry_on[:, None, None] * carried
    normed = numerator * lax.rsqrt(jnp.mean(numerator * numerator, axis=-1, keepdims=True) + 1e-06)
    gain_heads = norm_gain.reshape(heads_here, HEAD)
    hidden = (normed * gain_heads[None]).astype(jnp.bfloat16).reshape(rows_here, width_here)
    return project_gathered(hidden, out_weight, "mp").astype(jnp.bfloat16)


def solution(mesh):
    in_specs = (
        P(("dp", "ctx"), "mp"),
        P(("dp", "ctx"), "mp"),
        P(("dp", "ctx"), "mp"),
        P(("dp", "ctx")),
        P("mp"),
        P(None, "mp"),
    )
    out_specs = P(("dp", "ctx"), "mp")
    return jax.shard_map(
        per_device, mesh=mesh, in_specs=in_specs, out_specs=out_specs, check_vma=False
    )
```

```python
import jax
import jax.numpy as jnp
from jax import lax
from jax.sharding import PartitionSpec as P

HEAD = 128


def features(raw_input):
    return (jax.nn.elu(raw_input.astype(jnp.float32)) + 1.0).astype(jnp.bfloat16)


def carried_in(local_sum, final_seg, axis):
    count = lax.axis_size(axis)
    shape = local_sum.shape
    flat = local_sum.reshape(count, -1)
    width = flat.shape[1]
    seg_row = jnp.full((count, HEAD), final_seg.astype(jnp.float32))
    sent = jnp.concatenate([flat, seg_row], axis=1)
    pieces = lax.all_to_all(sent, axis, 0, 0, tiled=True)
    sums = pieces[:, :width]
    segs = pieces[:, width]
    block = jnp.arange(count)
    prev_seg = jnp.concatenate([jnp.full((1,), -1.0, jnp.float32), segs[:-1]])
    mask = (block[None, :] < block[:, None]) & (segs[None, :] == prev_seg[:, None])
    carry = jnp.sum(jnp.where(mask[:, :, None], sums[None, :, :], 0.0), axis=1)
    back = jnp.concatenate([carry, jnp.broadcast_to(prev_seg[:, None], (count, HEAD))], axis=1)
    mine = lax.all_to_all(back, axis, 0, 0, tiled=True)
    before_sum = mine[:, :width].reshape(shape)
    before_seg = mine[0, width]
    return before_sum, before_seg


def project_gathered(hidden, out_weight, axis):
    count, mine = lax.axis_size(axis), lax.axis_index(axis)
    rows, width = hidden.shape
    half = rows // 2
    weight_groups = out_weight.reshape(count, width, out_weight.shape[1])
    ahead = [(j, (j + 1) % count) for j in range(count)]
    behind = [(j, (j - 1) % count) for j in range(count)]

    def part(block, offset):
        group = lax.rem(mine + offset + count, count)
        return jnp.dot(block, weight_groups[group], preferred_element_type=jnp.float32)

    top, bottom = hidden[:half], hidden[half:]
    left_top = lax.ppermute(top, axis, ahead)
    right_bottom = lax.ppermute(bottom, axis, behind)
    left_top, right_bottom, top_later, bottom_later = lax.optimization_barrier(
        (left_top, right_bottom, top, bottom)
    )
    left_bottom = lax.ppermute(bottom_later, axis, ahead)
    right_top = lax.ppermute(top_later, axis, behind)
    far_top = lax.ppermute(left_top, axis, ahead)
    far_bottom = lax.ppermute(right_bottom, axis, behind)
    out_top = part(top, 0) + part(left_top, -1) + part(right_top, 1) + part(far_top, 2)
    out_bottom = (
        part(bottom, 0) + part(right_bottom, 1) + part(left_bottom, -1) + part(far_bottom, 2)
    )
    return jnp.concatenate([out_top, out_bottom], axis=0)


def per_device(queries, keys, values, segment_ids, norm_gain, out_weight):
    rows_here = queries.shape[0]
    width_here = queries.shape[1]
    heads_here = width_here // HEAD
    feat_query = features(queries).reshape(rows_here, heads_here, HEAD)
    feat_key = features(keys).reshape(rows_here, heads_here, HEAD)
    value_heads = values.reshape(rows_here, heads_here, HEAD)
    final_seg = segment_ids[rows_here - 1]
    in_final = (segment_ids == final_seg).astype(jnp.bfloat16)
    local_sum = jnp.einsum(
        "thd,the->hde",
        feat_key * in_final[:, None, None],
        value_heads,
        preferred_element_type=jnp.float32,
    )
    before_sum, before_seg = carried_in(local_sum, final_seg, "ctx")
    position = jnp.arange(rows_here)
    allowed = (position[None, :] <= position[:, None]) & (
        segment_ids[:, None] == segment_ids[None, :]
    )
    scores = jnp.einsum("thd,shd->hts", feat_query, feat_key, preferred_element_type=jnp.float32)
    weights = jnp.where(allowed[None], scores, 0.0).astype(jnp.bfloat16)
    inside = jnp.einsum("hts,she->the", weights, value_heads, preferred_element_type=jnp.float32)
    state_hi = before_sum.astype(jnp.bfloat16)
    state_lo = (before_sum - state_hi.astype(jnp.float32)).astype(jnp.bfloat16)
    carried = jnp.einsum(
        "thd,hde->the", feat_query, state_hi, preferred_element_type=jnp.float32
    ) + jnp.einsum("thd,hde->the", feat_query, state_lo, preferred_element_type=jnp.float32)
    carry_on = (segment_ids.astype(jnp.float32) == before_seg).astype(jnp.float32)
    numerator = inside + carry_on[:, None, None] * carried
    normed = numerator * lax.rsqrt(jnp.mean(numerator * numerator, axis=-1, keepdims=True) + 1e-06)
    gain_heads = norm_gain.reshape(heads_here, HEAD)
    hidden = (normed * gain_heads[None]).astype(jnp.bfloat16).reshape(rows_here, width_here)
    return project_gathered(hidden, out_weight, "mp").astype(jnp.bfloat16)


def solution(mesh):
    in_specs = (
        P(("dp", "ctx"), "mp"),
        P(("dp", "ctx"), "mp"),
        P(("dp", "ctx"), "mp"),
        P(("dp", "ctx")),
        P("mp"),
        P(None, "mp"),
    )
    out_specs = P(("dp", "ctx"), "mp")
    return jax.shard_map(
        per_device, mesh=mesh, in_specs=in_specs, out_specs=out_specs, check_vma=False
    )
```

```python
import jax
import jax.numpy as jnp
from jax import lax
from jax.sharding import PartitionSpec as P

HEAD = 128


def features(raw_input):
    return (jax.nn.elu(raw_input.astype(jnp.float32)) + 1.0).astype(jnp.bfloat16)


def carried_in(local_sum, final_seg, axis):
    count = lax.axis_size(axis)
    shape = local_sum.shape
    tile = local_sum.size // (count * HEAD)
    flat = local_sum.reshape(count, tile, HEAD)
    seg_rows = jnp.full((count, 8, HEAD), final_seg.astype(jnp.float32))
    sent = jnp.concatenate([flat, seg_rows], axis=1)
    pieces = lax.all_to_all(sent, axis, 0, 0, tiled=True)
    sums = pieces[:, :tile]
    segs = pieces[:, tile, 0]
    block = jnp.arange(count)
    prev_seg = jnp.concatenate([jnp.full((1,), -1.0, jnp.float32), segs[:-1]])
    mask = (block[None, :] < block[:, None]) & (segs[None, :] == prev_seg[:, None])
    carry = jnp.sum(jnp.where(mask[:, :, None, None], sums[None], 0.0), axis=1)
    back = jnp.concatenate(
        [carry, jnp.broadcast_to(prev_seg[:, None, None], (count, 8, HEAD))], axis=1
    )
    mine = lax.all_to_all(back, axis, 0, 0, tiled=True)
    before_sum = mine[:, :tile].reshape(shape)
    before_seg = mine[0, tile, 0]
    return before_sum, before_seg


def project_gathered(hidden, out_weight, axis):
    count, mine = lax.axis_size(axis), lax.axis_index(axis)
    rows, width = hidden.shape
    half = rows // 2
    weight_groups = out_weight.reshape(count, width, out_weight.shape[1])
    ahead = [(j, (j + 1) % count) for j in range(count)]
    behind = [(j, (j - 1) % count) for j in range(count)]

    def part(block, offset):
        group = lax.rem(mine + offset + count, count)
        return jnp.dot(block, weight_groups[group], preferred_element_type=jnp.float32)

    top, bottom = hidden[:half], hidden[half:]
    left_top = lax.ppermute(top, axis, ahead)
    right_bottom = lax.ppermute(bottom, axis, behind)
    left_top, right_bottom, top_later, bottom_later = lax.optimization_barrier(
        (left_top, right_bottom, top, bottom)
    )
    left_bottom = lax.ppermute(bottom_later, axis, ahead)
    right_top = lax.ppermute(top_later, axis, behind)
    far_top = lax.ppermute(left_top, axis, ahead)
    far_bottom = lax.ppermute(right_bottom, axis, behind)
    own = jnp.concatenate([part(top, 0), part(bottom, 0)], axis=0)
    left = jnp.concatenate([part(left_top, -1), part(left_bottom, -1)], axis=0)
    right = jnp.concatenate([part(right_top, 1), part(right_bottom, 1)], axis=0)
    far = jnp.concatenate([part(far_top, 2), part(far_bottom, 2)], axis=0)
    return own + left + right + far


def per_device(queries, keys, values, segment_ids, norm_gain, out_weight):
    rows_here = queries.shape[0]
    width_here = queries.shape[1]
    heads_here = width_here // HEAD
    feat_query = features(queries).reshape(rows_here, heads_here, HEAD)
    feat_key = features(keys).reshape(rows_here, heads_here, HEAD)
    value_heads = values.reshape(rows_here, heads_here, HEAD)
    final_seg = segment_ids[rows_here - 1]
    in_final = (segment_ids == final_seg).astype(jnp.bfloat16)
    local_sum = jnp.einsum(
        "thd,the->hde",
        feat_key * in_final[:, None, None],
        value_heads,
        preferred_element_type=jnp.float32,
    )
    before_sum, before_seg = carried_in(local_sum, final_seg, "ctx")
    position = jnp.arange(rows_here)
    allowed = (position[None, :] <= position[:, None]) & (
        segment_ids[:, None] == segment_ids[None, :]
    )
    scores = jnp.einsum("thd,shd->hts", feat_query, feat_key, preferred_element_type=jnp.float32)
    weights = jnp.where(allowed[None], scores, 0.0).astype(jnp.bfloat16)
    inside = jnp.einsum("hts,she->the", weights, value_heads, preferred_element_type=jnp.float32)
    state_hi = before_sum.astype(jnp.bfloat16)
    state_lo = (before_sum - state_hi.astype(jnp.float32)).astype(jnp.bfloat16)
    carried = jnp.einsum(
        "thd,hde->the", feat_query, state_hi, preferred_element_type=jnp.float32
    ) + jnp.einsum("thd,hde->the", feat_query, state_lo, preferred_element_type=jnp.float32)
    carry_on = (segment_ids.astype(jnp.float32) == before_seg).astype(jnp.float32)
    numerator = inside + carry_on[:, None, None] * carried
    normed = numerator * lax.rsqrt(jnp.mean(numerator * numerator, axis=-1, keepdims=True) + 1e-06)
    gain_heads = norm_gain.reshape(heads_here, HEAD)
    hidden = (normed * gain_heads[None]).astype(jnp.bfloat16).reshape(rows_here, width_here)
    return project_gathered(hidden, out_weight, "mp").astype(jnp.bfloat16)


def solution(mesh):
    in_specs = (
        P(("dp", "ctx"), "mp"),
        P(("dp", "ctx"), "mp"),
        P(("dp", "ctx"), "mp"),
        P(("dp", "ctx")),
        P("mp"),
        P(None, "mp"),
    )
    out_specs = P(("dp", "ctx"), "mp")
    return jax.shard_map(
        per_device, mesh=mesh, in_specs=in_specs, out_specs=out_specs, check_vma=False
    )
```

```python
import jax
import jax.numpy as jnp
from jax import lax
from jax.sharding import PartitionSpec as P

HEAD = 128


def features(raw_input):
    return (jax.nn.elu(raw_input.astype(jnp.float32)) + 1.0).astype(jnp.bfloat16)


def join(early_sum, early_seg, later_sum, later_seg):
    return later_sum + jnp.where(early_seg == later_seg, early_sum, 0.0)


def carried_in(local_sum, final_seg, chips, cores):
    count = lax.axis_size(chips)
    core = lax.axis_index(cores)
    shape = local_sum.shape
    flat = local_sum.reshape(2, -1, HEAD)
    seg = final_seg.astype(jnp.float32)
    swap = [(0, 1), (1, 0)]
    other_sum, other_seg = lax.ppermute((flat, seg), cores, swap)
    first_sum = jnp.where(core == 0, flat, other_sum)
    first_seg = jnp.where(core == 0, seg, other_seg)
    last_sum = jnp.where(core == 0, other_sum, flat)
    last_seg = jnp.where(core == 0, other_seg, seg)
    chip_sum = join(first_sum, first_seg, last_sum, last_seg)[core]
    tile = chip_sum.shape[0] // count
    seg_rows = jnp.full((count, 8, HEAD), last_seg)
    sent = jnp.concatenate([chip_sum.reshape(count, tile, HEAD), seg_rows], axis=1)
    pieces = lax.all_to_all(sent, chips, 0, 0, tiled=True)
    sums = pieces[:, :tile]
    segs = pieces[:, tile, 0]
    block = jnp.arange(count)
    prev_seg = jnp.concatenate([jnp.full((1,), -1.0, jnp.float32), segs[:-1]])
    mask = (block[None, :] < block[:, None]) & (segs[None, :] == prev_seg[:, None])
    carry = jnp.sum(jnp.where(mask[:, :, None, None], sums[None], 0.0), axis=1)
    back = jnp.concatenate(
        [carry, jnp.broadcast_to(prev_seg[:, None, None], (count, 8, HEAD))], axis=1
    )
    mine = lax.all_to_all(back, chips, 0, 0, tiled=True)
    half_sum = mine[:, :tile].reshape(-1, HEAD)
    chip_seg = mine[0, tile, 0]
    other_half = lax.ppermute(half_sum, cores, swap)
    before_chip = jnp.where(
        core == 0,
        jnp.stack([half_sum, other_half]),
        jnp.stack([other_half, half_sum]),
    )
    before_sum = jnp.where(
        core == 0, before_chip, join(before_chip, chip_seg, first_sum, first_seg)
    ).reshape(shape)
    before_seg = jnp.where(core == 0, chip_seg, first_seg)
    return before_sum, before_seg


def project_gathered(hidden, out_weight, axis):
    count, mine = lax.axis_size(axis), lax.axis_index(axis)
    rows, width = hidden.shape
    half = rows // 2
    weight_groups = out_weight.reshape(count, width, out_weight.shape[1])
    ahead = [(j, (j + 1) % count) for j in range(count)]
    behind = [(j, (j - 1) % count) for j in range(count)]

    def part(block, offset):
        group = lax.rem(mine + offset + count, count)
        return jnp.dot(block, weight_groups[group], preferred_element_type=jnp.float32)

    top, bottom = hidden[:half], hidden[half:]
    left_top = lax.ppermute(top, axis, ahead)
    right_bottom = lax.ppermute(bottom, axis, behind)
    left_top, right_bottom, top_later, bottom_later = lax.optimization_barrier(
        (left_top, right_bottom, top, bottom)
    )
    left_bottom = lax.ppermute(bottom_later, axis, ahead)
    right_top = lax.ppermute(top_later, axis, behind)
    far_top = lax.ppermute(left_top, axis, ahead)
    far_bottom = lax.ppermute(right_bottom, axis, behind)
    out_top = part(top, 0) + part(left_top, -1) + part(right_top, 1) + part(far_top, 2)
    out_bottom = (
        part(bottom, 0) + part(right_bottom, 1) + part(left_bottom, -1) + part(far_bottom, 2)
    )
    return jnp.concatenate([out_top, out_bottom], axis=0)


def per_device(queries, keys, values, segment_ids, norm_gain, out_weight):
    rows_here = queries.shape[0]
    width_here = queries.shape[1]
    heads_here = width_here // HEAD
    feat_query = features(queries).reshape(rows_here, heads_here, HEAD)
    feat_key = features(keys).reshape(rows_here, heads_here, HEAD)
    value_heads = values.reshape(rows_here, heads_here, HEAD)
    final_seg = segment_ids[rows_here - 1]
    in_final = (segment_ids == final_seg).astype(jnp.bfloat16)
    local_sum = jnp.einsum(
        "thd,the->hde",
        feat_key * in_final[:, None, None],
        value_heads,
        preferred_element_type=jnp.float32,
    )
    before_sum, before_seg = carried_in(local_sum, final_seg, "cz", "cc")
    position = jnp.arange(rows_here)
    allowed = (position[None, :] <= position[:, None]) & (
        segment_ids[:, None] == segment_ids[None, :]
    )
    scores = jnp.einsum("thd,shd->hts", feat_query, feat_key, preferred_element_type=jnp.float32)
    weights = jnp.where(allowed[None], scores, 0.0).astype(jnp.bfloat16)
    inside = jnp.einsum("hts,she->the", weights, value_heads, preferred_element_type=jnp.float32)
    state_hi = before_sum.astype(jnp.bfloat16)
    state_lo = (before_sum - state_hi.astype(jnp.float32)).astype(jnp.bfloat16)
    carried = jnp.einsum(
        "thd,hde->the", feat_query, state_hi, preferred_element_type=jnp.float32
    ) + jnp.einsum("thd,hde->the", feat_query, state_lo, preferred_element_type=jnp.float32)
    carry_on = (segment_ids.astype(jnp.float32) == before_seg).astype(jnp.float32)
    numerator = inside + carry_on[:, None, None] * carried
    normed = numerator * lax.rsqrt(jnp.mean(numerator * numerator, axis=-1, keepdims=True) + 1e-06)
    gain_heads = norm_gain.reshape(heads_here, HEAD)
    hidden = (normed * gain_heads[None]).astype(jnp.bfloat16).reshape(rows_here, width_here)
    return project_gathered(hidden, out_weight, "mp").astype(jnp.bfloat16)


def solution(mesh):
    dp, ctx, mp = (mesh.shape[name] for name in ("dp", "ctx", "mp"))
    split = jax.sharding.Mesh(
        mesh.devices.reshape(dp, ctx // 2, 2, mp), ("dp", "cz", "cc", "mp")
    )
    rows = ("dp", "cz", "cc")
    in_specs = (
        P(rows, "mp"),
        P(rows, "mp"),
        P(rows, "mp"),
        P(rows),
        P("mp"),
        P(None, "mp"),
    )
    out_specs = P(rows, "mp")
    return jax.shard_map(
        per_device, mesh=split, in_specs=in_specs, out_specs=out_specs, check_vma=False
    )
```

```python
import jax
import jax.numpy as jnp
from jax import lax
from jax.sharding import PartitionSpec as P

HEAD = 128


def features(raw_input):
    return (jax.nn.elu(raw_input.astype(jnp.float32)) + 1.0).astype(jnp.bfloat16)


def carried_in(local_sum, final_seg, first_seg, axis):
    count = lax.axis_size(axis)
    shape = local_sum.shape
    tile = local_sum.size // (count * HEAD)
    flat = local_sum.reshape(count, tile, HEAD)
    seg_rows = jnp.concatenate(
        [
            jnp.full((count, 1, HEAD), final_seg.astype(jnp.float32)),
            jnp.full((count, 7, HEAD), first_seg.astype(jnp.float32)),
        ],
        axis=1,
    )
    sent = jnp.concatenate([flat, seg_rows], axis=1)
    pieces = lax.all_to_all(sent, axis, 0, 0, tiled=True)
    sums = pieces[:, :tile]
    last_segs = pieces[:, tile, 0]
    first_segs = pieces[:, tile + 1, 0]
    block = jnp.arange(count)
    mask = (block[None, :] < block[:, None]) & (last_segs[None, :] == first_segs[:, None])
    carry = jnp.sum(jnp.where(mask[:, :, None, None], sums[None], 0.0), axis=1)
    return lax.all_to_all(carry, axis, 0, 0, tiled=True).reshape(shape)


def project_gathered(hidden, out_weight, axis):
    count, mine = lax.axis_size(axis), lax.axis_index(axis)
    rows, width = hidden.shape
    half = rows // 2
    weight_groups = out_weight.reshape(count, width, out_weight.shape[1])
    ahead = [(j, (j + 1) % count) for j in range(count)]
    behind = [(j, (j - 1) % count) for j in range(count)]

    def part(block, offset):
        group = lax.rem(mine + offset + count, count)
        return jnp.dot(block, weight_groups[group], preferred_element_type=jnp.float32)

    top, bottom = hidden[:half], hidden[half:]
    left_top = lax.ppermute(top, axis, ahead)
    right_bottom = lax.ppermute(bottom, axis, behind)
    left_top, right_bottom, top_later, bottom_later = lax.optimization_barrier(
        (left_top, right_bottom, top, bottom)
    )
    left_bottom = lax.ppermute(bottom_later, axis, ahead)
    right_top = lax.ppermute(top_later, axis, behind)
    far_top = lax.ppermute(left_top, axis, ahead)
    far_bottom = lax.ppermute(right_bottom, axis, behind)
    out_top = part(top, 0) + part(left_top, -1) + part(right_top, 1) + part(far_top, 2)
    out_bottom = (
        part(bottom, 0) + part(right_bottom, 1) + part(left_bottom, -1) + part(far_bottom, 2)
    )
    return jnp.concatenate([out_top, out_bottom], axis=0)


def per_device(queries, keys, values, segment_ids, norm_gain, out_weight):
    rows_here = queries.shape[0]
    width_here = queries.shape[1]
    heads_here = width_here // HEAD
    feat_query = lax.optimization_barrier(features(queries)).reshape(rows_here, heads_here, HEAD)
    feat_key = features(keys).reshape(rows_here, heads_here, HEAD)
    value_heads = values.reshape(rows_here, heads_here, HEAD)
    final_seg = segment_ids[rows_here - 1]
    in_final = (segment_ids == final_seg).astype(jnp.bfloat16)
    local_sum = jnp.einsum(
        "thd,the->hde",
        feat_key * in_final[:, None, None],
        value_heads,
        preferred_element_type=jnp.float32,
    )
    before_sum = carried_in(local_sum, final_seg, segment_ids[0], "ctx")
    position = jnp.arange(rows_here)
    allowed = (position[None, :] <= position[:, None]) & (
        segment_ids[:, None] == segment_ids[None, :]
    )
    scores = jnp.einsum("thd,shd->hts", feat_query, feat_key, preferred_element_type=jnp.float32)
    weights = jnp.where(allowed[None], scores, 0.0).astype(jnp.bfloat16)
    inside = jnp.einsum("hts,she->the", weights, value_heads, preferred_element_type=jnp.float32)
    state_hi = before_sum.astype(jnp.bfloat16)
    state_lo = (before_sum - state_hi.astype(jnp.float32)).astype(jnp.bfloat16)
    carried = jnp.einsum(
        "thd,hde->the", feat_query, state_hi, preferred_element_type=jnp.float32
    ) + jnp.einsum("thd,hde->the", feat_query, state_lo, preferred_element_type=jnp.float32)
    carry_on = (segment_ids == segment_ids[0]).astype(jnp.float32)
    numerator = inside + carry_on[:, None, None] * carried
    normed = numerator * lax.rsqrt(jnp.mean(numerator * numerator, axis=-1, keepdims=True) + 1e-06)
    gain_heads = norm_gain.reshape(heads_here, HEAD)
    hidden = (normed * gain_heads[None]).astype(jnp.bfloat16).reshape(rows_here, width_here)
    return project_gathered(hidden, out_weight, "mp").astype(jnp.bfloat16)


def solution(mesh):
    in_specs = (
        P(("dp", "ctx"), "mp"),
        P(("dp", "ctx"), "mp"),
        P(("dp", "ctx"), "mp"),
        P(("dp", "ctx")),
        P("mp"),
        P(None, "mp"),
    )
    out_specs = P(("dp", "ctx"), "mp")
    return jax.shard_map(
        per_device, mesh=mesh, in_specs=in_specs, out_specs=out_specs, check_vma=False
    )
```

```python
import jax
import jax.numpy as jnp
from jax import lax
from jax.sharding import PartitionSpec as P

HEAD = 128


def features(raw_input):
    return (jax.nn.elu(raw_input.astype(jnp.float32)) + 1.0).astype(jnp.bfloat16)


def carried_in(local_sum, final_seg, first_seg, axis):
    count = lax.axis_size(axis)
    shape = local_sum.shape
    tile = local_sum.size // (count * HEAD)
    flat = local_sum.reshape(count, tile, HEAD)
    seg_rows = jnp.concatenate(
        [
            jnp.full((count, 1, HEAD), final_seg.astype(jnp.float32)),
            jnp.full((count, 7, HEAD), first_seg.astype(jnp.float32)),
        ],
        axis=1,
    )
    sent = jnp.concatenate([flat, seg_rows], axis=1)
    pieces = lax.all_to_all(sent, axis, 0, 0, tiled=True)
    sums = pieces[:, :tile]
    last_segs = pieces[:, tile, 0]
    first_segs = pieces[:, tile + 1, 0]
    block = jnp.arange(count)
    mask = (block[None, :] < block[:, None]) & (last_segs[None, :] == first_segs[:, None])
    carry = jnp.sum(jnp.where(mask[:, :, None, None], sums[None], 0.0), axis=1)
    return lax.all_to_all(carry, axis, 0, 0, tiled=True).reshape(shape)


def project_gathered(hidden, out_weight, axis):
    count, mine = lax.axis_size(axis), lax.axis_index(axis)
    rows, width = hidden.shape
    half = width // 2
    weight_halves = out_weight.reshape(count, 2, half, out_weight.shape[1])
    ahead = [(j, (j + 1) % count) for j in range(count)]
    behind = [(j, (j - 1) % count) for j in range(count)]

    def part(block, offset, which):
        group = lax.rem(mine + offset + count, count)
        return jnp.dot(block, weight_halves[group, which], preferred_element_type=jnp.float32)

    first, second = hidden[:, :half], hidden[:, half:]
    left_first = lax.ppermute(first, axis, ahead)
    right_second = lax.ppermute(second, axis, behind)
    left_first, right_second, first_later, second_later = lax.optimization_barrier(
        (left_first, right_second, first, second)
    )
    left_second = lax.ppermute(second_later, axis, ahead)
    right_first = lax.ppermute(first_later, axis, behind)
    far_first = lax.ppermute(left_first, axis, ahead)
    far_second = lax.ppermute(right_second, axis, behind)
    total = jnp.dot(hidden, out_weight.reshape(count, width, -1)[mine], preferred_element_type=jnp.float32)
    for block, offset, which in (
        (left_first, -1, 0),
        (right_second, 1, 1),
        (left_second, -1, 1),
        (right_first, 1, 0),
        (far_first, 2, 0),
    ):
        total = lax.optimization_barrier(total + part(block, offset, which))
    return total + part(far_second, 2, 1)


def per_device(queries, keys, values, segment_ids, norm_gain, out_weight):
    rows_here = queries.shape[0]
    width_here = queries.shape[1]
    heads_here = width_here // HEAD
    feat_query = lax.optimization_barrier(features(queries)).reshape(rows_here, heads_here, HEAD)
    feat_key = features(keys).reshape(rows_here, heads_here, HEAD)
    value_heads = values.reshape(rows_here, heads_here, HEAD)
    final_seg = segment_ids[rows_here - 1]
    in_final = (segment_ids == final_seg).astype(jnp.bfloat16)
    local_sum = jnp.einsum(
        "thd,the->hde",
        feat_key * in_final[:, None, None],
        value_heads,
        preferred_element_type=jnp.float32,
    )
    before_sum = carried_in(local_sum, final_seg, segment_ids[0], "ctx")
    position = jnp.arange(rows_here)
    allowed = (position[None, :] <= position[:, None]) & (
        segment_ids[:, None] == segment_ids[None, :]
    )
    scores = jnp.einsum("thd,shd->hts", feat_query, feat_key, preferred_element_type=jnp.float32)
    weights = jnp.where(allowed[None], scores, 0.0).astype(jnp.bfloat16)
    inside = jnp.einsum("hts,she->the", weights, value_heads, preferred_element_type=jnp.float32)
    state_hi = before_sum.astype(jnp.bfloat16)
    state_lo = (before_sum - state_hi.astype(jnp.float32)).astype(jnp.bfloat16)
    carried = jnp.einsum(
        "thd,hde->the", feat_query, state_hi, preferred_element_type=jnp.float32
    ) + jnp.einsum("thd,hde->the", feat_query, state_lo, preferred_element_type=jnp.float32)
    carry_on = (segment_ids == segment_ids[0]).astype(jnp.float32)
    numerator = inside + carry_on[:, None, None] * carried
    normed = numerator * lax.rsqrt(jnp.mean(numerator * numerator, axis=-1, keepdims=True) + 1e-06)
    gain_heads = norm_gain.reshape(heads_here, HEAD)
    hidden = (normed * gain_heads[None]).astype(jnp.bfloat16).reshape(rows_here, width_here)
    return project_gathered(hidden, out_weight, "mp").astype(jnp.bfloat16)


def solution(mesh):
    in_specs = (
        P(("dp", "ctx"), "mp"),
        P(("dp", "ctx"), "mp"),
        P(("dp", "ctx"), "mp"),
        P(("dp", "ctx")),
        P("mp"),
        P(None, "mp"),
    )
    out_specs = P(("dp", "ctx"), "mp")
    return jax.shard_map(
        per_device, mesh=mesh, in_specs=in_specs, out_specs=out_specs, check_vma=False
    )
```

```python
import jax
import jax.numpy as jnp
from jax import lax
from jax.sharding import PartitionSpec as P

HEAD = 128


def features(raw_input):
    return (jax.nn.elu(raw_input.astype(jnp.float32)) + 1.0).astype(jnp.bfloat16)


def carried_in(local_sum, final_seg, first_seg, axis):
    count = lax.axis_size(axis)
    shape = local_sum.shape
    tile = local_sum.size // (count * HEAD)
    flat = local_sum.reshape(count, tile, HEAD)
    seg_rows = jnp.concatenate(
        [
            jnp.full((count, 1, HEAD), final_seg.astype(jnp.float32)),
            jnp.full((count, 7, HEAD), first_seg.astype(jnp.float32)),
        ],
        axis=1,
    )
    sent = jnp.concatenate([flat, seg_rows], axis=1)
    pieces = lax.all_to_all(sent, axis, 0, 0, tiled=True)
    sums = pieces[:, :tile]
    last_segs = pieces[:, tile, 0]
    first_segs = pieces[:, tile + 1, 0]
    block = jnp.arange(count)
    mask = (block[None, :] < block[:, None]) & (last_segs[None, :] == first_segs[:, None])
    carry = jnp.sum(jnp.where(mask[:, :, None, None], sums[None], 0.0), axis=1)
    return lax.all_to_all(carry, axis, 0, 0, tiled=True).reshape(shape)


def project_gathered(hidden, out_weight, axis):
    count, mine = lax.axis_size(axis), lax.axis_index(axis)
    rows, width = hidden.shape
    half = width // 2
    weight_halves = out_weight.reshape(count, 2, half, out_weight.shape[1])
    ahead = [(j, (j + 1) % count) for j in range(count)]
    behind = [(j, (j - 1) % count) for j in range(count)]

    def part(block, offset, which):
        group = lax.rem(mine + offset + count, count)
        return jnp.dot(block, weight_halves[group, which], preferred_element_type=jnp.float32)

    first, second = hidden[:, :half], hidden[:, half:]
    left_first = lax.ppermute(first, axis, ahead)
    right_second = lax.ppermute(second, axis, behind)
    left_first, right_second, first_later, second_later = lax.optimization_barrier(
        (left_first, right_second, first, second)
    )
    left_second = lax.ppermute(second_later, axis, ahead)
    right_first = lax.ppermute(first_later, axis, behind)
    far_first = lax.ppermute(left_first, axis, ahead)
    far_second = lax.ppermute(right_second, axis, behind)
    total = jnp.dot(hidden, out_weight.reshape(count, width, -1)[mine], preferred_element_type=jnp.float32)
    for block, offset, which in (
        (left_first, -1, 0),
        (right_second, 1, 1),
        (left_second, -1, 1),
        (right_first, 1, 0),
        (far_first, 2, 0),
    ):
        total = lax.optimization_barrier(total + part(block, offset, which))
    return total + part(far_second, 2, 1)


def per_device(queries, keys, values, segment_ids, norm_gain, out_weight):
    rows_here = queries.shape[0]
    width_here = queries.shape[1]
    heads_here = width_here // HEAD
    feat_query = lax.optimization_barrier(features(queries)).reshape(rows_here, heads_here, HEAD)
    feat_key = features(keys).reshape(rows_here, heads_here, HEAD)
    value_heads = values.reshape(rows_here, heads_here, HEAD)
    final_seg = segment_ids[rows_here - 1]
    in_final = (segment_ids == final_seg).astype(jnp.bfloat16)
    local_sum = jnp.einsum(
        "the,thd->hed",
        value_heads,
        feat_key * in_final[:, None, None],
        preferred_element_type=jnp.float32,
    )
    before_sum = carried_in(local_sum, final_seg, segment_ids[0], "ctx")
    position = jnp.arange(rows_here)
    allowed = (position[None, :] <= position[:, None]) & (
        segment_ids[:, None] == segment_ids[None, :]
    )
    scores = jnp.einsum("thd,shd->hts", feat_query, feat_key, preferred_element_type=jnp.float32)
    weights = jnp.where(allowed[None], scores, 0.0).astype(jnp.bfloat16)
    inside = jnp.einsum("hts,she->the", weights, value_heads, preferred_element_type=jnp.float32)
    state_hi = before_sum.astype(jnp.bfloat16)
    state_lo = (before_sum - state_hi.astype(jnp.float32)).astype(jnp.bfloat16)
    carried = jnp.einsum(
        "thd,hed->the", feat_query, state_hi, preferred_element_type=jnp.float32
    ) + jnp.einsum("thd,hed->the", feat_query, state_lo, preferred_element_type=jnp.float32)
    carry_on = (segment_ids == segment_ids[0]).astype(jnp.float32)
    numerator = inside + carry_on[:, None, None] * carried
    normed = numerator * lax.rsqrt(jnp.mean(numerator * numerator, axis=-1, keepdims=True) + 1e-06)
    gain_heads = norm_gain.reshape(heads_here, HEAD)
    hidden = (normed * gain_heads[None]).astype(jnp.bfloat16).reshape(rows_here, width_here)
    return project_gathered(hidden, out_weight, "mp").astype(jnp.bfloat16)


def solution(mesh):
    in_specs = (
        P(("dp", "ctx"), "mp"),
        P(("dp", "ctx"), "mp"),
        P(("dp", "ctx"), "mp"),
        P(("dp", "ctx")),
        P("mp"),
        P(None, "mp"),
    )
    out_specs = P(("dp", "ctx"), "mp")
    return jax.shard_map(
        per_device, mesh=mesh, in_specs=in_specs, out_specs=out_specs, check_vma=False
    )
```

```python
import jax
import jax.numpy as jnp
from jax import lax
from jax.sharding import PartitionSpec as P

HEAD = 128


def features(raw_input):
    return (jax.nn.elu(raw_input.astype(jnp.float32)) + 1.0).astype(jnp.bfloat16)


def carried_in(local_sum, final_seg, first_seg, axis):
    count = lax.axis_size(axis)
    shape = local_sum.shape
    tile = local_sum.size // (count * HEAD)
    flat = local_sum.reshape(count, tile, HEAD)
    seg_rows = jnp.concatenate(
        [
            jnp.full((count, 1, HEAD), final_seg.astype(jnp.float32)),
            jnp.full((count, 7, HEAD), first_seg.astype(jnp.float32)),
        ],
        axis=1,
    )
    sent = jnp.concatenate([flat, seg_rows], axis=1)
    pieces = lax.all_to_all(sent, axis, 0, 0, tiled=True)
    sums = pieces[:, :tile]
    last_segs = pieces[:, tile, 0]
    first_segs = pieces[:, tile + 1, 0]
    block = jnp.arange(count)
    mask = (block[None, :] < block[:, None]) & (last_segs[None, :] == first_segs[:, None])
    carry = jnp.sum(jnp.where(mask[:, :, None, None], sums[None], 0.0), axis=1)
    return lax.all_to_all(carry, axis, 0, 0, tiled=True).reshape(shape)


def project_gathered(hidden, out_weight, axis):
    count, mine = lax.axis_size(axis), lax.axis_index(axis)
    rows, width = hidden.shape
    half = width // 2
    weight_halves = out_weight.reshape(count, 2, half, out_weight.shape[1])
    ahead = [(j, (j + 1) % count) for j in range(count)]
    behind = [(j, (j - 1) % count) for j in range(count)]

    def rows_of(offset, which):
        return weight_halves[lax.rem(mine + offset + count, count), which]

    def dot(block, weight):
        return jnp.dot(block, weight, preferred_element_type=jnp.float32)

    first, second = hidden[:, :half], hidden[:, half:]
    left_first = lax.ppermute(first, axis, ahead)
    right_second = lax.ppermute(second, axis, behind)
    from_left = lax.ppermute(jnp.concatenate([second, left_first], axis=1), axis, ahead)
    from_right = lax.ppermute(jnp.concatenate([first, right_second], axis=1), axis, behind)
    left_weight = jnp.concatenate([rows_of(-1, 1), rows_of(2, 0)], axis=0)
    right_weight = jnp.concatenate([rows_of(1, 0), rows_of(2, 1)], axis=0)
    total = dot(hidden, out_weight.reshape(count, width, -1)[mine])
    total = total + dot(left_first, rows_of(-1, 0)) + dot(right_second, rows_of(1, 1))
    return total + dot(from_left, left_weight) + dot(from_right, right_weight)


def per_device(queries, keys, values, segment_ids, norm_gain, out_weight):
    rows_here = queries.shape[0]
    width_here = queries.shape[1]
    heads_here = width_here // HEAD
    feat_query = lax.optimization_barrier(features(queries)).reshape(rows_here, heads_here, HEAD)
    feat_key = features(keys).reshape(rows_here, heads_here, HEAD)
    value_heads = values.reshape(rows_here, heads_here, HEAD)
    final_seg = segment_ids[rows_here - 1]
    in_final = (segment_ids == final_seg).astype(jnp.bfloat16)
    local_sum = jnp.einsum(
        "the,thd->hed",
        value_heads,
        feat_key * in_final[:, None, None],
        preferred_element_type=jnp.float32,
    )
    before_sum = carried_in(local_sum, final_seg, segment_ids[0], "ctx")
    position = jnp.arange(rows_here)
    allowed = (position[None, :] <= position[:, None]) & (
        segment_ids[:, None] == segment_ids[None, :]
    )
    scores = jnp.einsum("thd,shd->hts", feat_query, feat_key, preferred_element_type=jnp.float32)
    weights = jnp.where(allowed[None], scores, 0.0).astype(jnp.bfloat16)
    inside = jnp.einsum("hts,she->the", weights, value_heads, preferred_element_type=jnp.float32)
    state_hi = before_sum.astype(jnp.bfloat16)
    state_lo = (before_sum - state_hi.astype(jnp.float32)).astype(jnp.bfloat16)
    carried = jnp.einsum(
        "thd,hed->the", feat_query, state_hi, preferred_element_type=jnp.float32
    ) + jnp.einsum("thd,hed->the", feat_query, state_lo, preferred_element_type=jnp.float32)
    carry_on = (segment_ids == segment_ids[0]).astype(jnp.float32)
    numerator = inside + carry_on[:, None, None] * carried
    normed = numerator * lax.rsqrt(jnp.mean(numerator * numerator, axis=-1, keepdims=True) + 1e-06)
    gain_heads = norm_gain.reshape(heads_here, HEAD)
    hidden = (normed * gain_heads[None]).astype(jnp.bfloat16).reshape(rows_here, width_here)
    return project_gathered(hidden, out_weight, "mp").astype(jnp.bfloat16)


def solution(mesh):
    in_specs = (
        P(("dp", "ctx"), "mp"),
        P(("dp", "ctx"), "mp"),
        P(("dp", "ctx"), "mp"),
        P(("dp", "ctx")),
        P("mp"),
        P(None, "mp"),
    )
    out_specs = P(("dp", "ctx"), "mp")
    return jax.shard_map(
        per_device, mesh=mesh, in_specs=in_specs, out_specs=out_specs, check_vma=False
    )
```

```python
import jax
import jax.numpy as jnp
from jax import lax
from jax.sharding import PartitionSpec as P

HEAD = 128


def features(raw_input):
    return (jax.nn.elu(raw_input.astype(jnp.float32)) + 1.0).astype(jnp.bfloat16)


def carried_in(local_sum, final_seg, first_seg, axis):
    count = lax.axis_size(axis)
    shape = local_sum.shape
    tile = local_sum.size // (count * HEAD)
    flat = local_sum.reshape(count, tile, HEAD)
    seg_rows = jnp.concatenate(
        [
            jnp.full((count, 1, HEAD), final_seg.astype(jnp.float32)),
            jnp.full((count, 7, HEAD), first_seg.astype(jnp.float32)),
        ],
        axis=1,
    )
    sent = jnp.concatenate([flat, seg_rows], axis=1)
    pieces = lax.all_to_all(sent, axis, 0, 0, tiled=True)
    sums = pieces[:, :tile]
    last_segs = pieces[:, tile, 0]
    first_segs = pieces[:, tile + 1, 0]
    block = jnp.arange(count)
    mask = (block[None, :] < block[:, None]) & (last_segs[None, :] == first_segs[:, None])
    carry = jnp.sum(jnp.where(mask[:, :, None, None], sums[None], 0.0), axis=1)
    return lax.all_to_all(carry, axis, 0, 0, tiled=True).reshape(shape)


def project_gathered(hidden, out_weight, axis):
    count, mine = lax.axis_size(axis), lax.axis_index(axis)
    rows, width = hidden.shape
    half = width // 2
    weight_halves = out_weight.reshape(count, 2, half, out_weight.shape[1])
    ahead = [(j, (j + 1) % count) for j in range(count)]
    behind = [(j, (j - 1) % count) for j in range(count)]

    def rows_of(offset, which):
        return weight_halves[lax.rem(mine + offset + count, count), which]

    def dot(block, weight):
        return jnp.dot(block, weight, preferred_element_type=jnp.float32)

    first, second = hidden[:, :half], hidden[:, half:]
    left_first = lax.ppermute(first, axis, ahead)
    right_second = lax.ppermute(second, axis, behind)
    from_left = lax.ppermute(jnp.concatenate([second, left_first], axis=1), axis, ahead)
    from_right = lax.ppermute(jnp.concatenate([first, right_second], axis=1), axis, behind)
    left_weight = jnp.concatenate([rows_of(-1, 1), rows_of(2, 0)], axis=0)
    right_weight = jnp.concatenate([rows_of(1, 0), rows_of(2, 1)], axis=0)
    total = dot(hidden, out_weight.reshape(count, width, -1)[mine])
    total = total + dot(left_first, rows_of(-1, 0)) + dot(right_second, rows_of(1, 1))
    total = lax.optimization_barrier(total)
    total = lax.optimization_barrier(total + dot(from_left, left_weight))
    return total + dot(from_right, right_weight)


def per_device(queries, keys, values, segment_ids, norm_gain, out_weight):
    rows_here = queries.shape[0]
    width_here = queries.shape[1]
    heads_here = width_here // HEAD
    feat_query = lax.optimization_barrier(features(queries)).reshape(rows_here, heads_here, HEAD)
    feat_key = features(keys).reshape(rows_here, heads_here, HEAD)
    value_heads = values.reshape(rows_here, heads_here, HEAD)
    final_seg = segment_ids[rows_here - 1]
    in_final = (segment_ids == final_seg).astype(jnp.bfloat16)
    local_sum = jnp.einsum(
        "the,thd->hed",
        value_heads,
        feat_key * in_final[:, None, None],
        preferred_element_type=jnp.float32,
    )
    before_sum = carried_in(local_sum, final_seg, segment_ids[0], "ctx")
    position = jnp.arange(rows_here)
    allowed = (position[None, :] <= position[:, None]) & (
        segment_ids[:, None] == segment_ids[None, :]
    )
    scores = jnp.einsum("thd,shd->hts", feat_query, feat_key, preferred_element_type=jnp.float32)
    weights = jnp.where(allowed[None], scores, 0.0).astype(jnp.bfloat16)
    inside = jnp.einsum("hts,she->the", weights, value_heads, preferred_element_type=jnp.float32)
    state_hi = before_sum.astype(jnp.bfloat16)
    state_lo = (before_sum - state_hi.astype(jnp.float32)).astype(jnp.bfloat16)
    carried = jnp.einsum(
        "thd,hed->the", feat_query, state_hi, preferred_element_type=jnp.float32
    ) + jnp.einsum("thd,hed->the", feat_query, state_lo, preferred_element_type=jnp.float32)
    carry_on = (segment_ids == segment_ids[0]).astype(jnp.float32)
    numerator = inside + carry_on[:, None, None] * carried
    normed = numerator * lax.rsqrt(jnp.mean(numerator * numerator, axis=-1, keepdims=True) + 1e-06)
    gain_heads = norm_gain.reshape(heads_here, HEAD)
    hidden = (normed * gain_heads[None]).astype(jnp.bfloat16).reshape(rows_here, width_here)
    return project_gathered(hidden, out_weight, "mp").astype(jnp.bfloat16)


def solution(mesh):
    in_specs = (
        P(("dp", "ctx"), "mp"),
        P(("dp", "ctx"), "mp"),
        P(("dp", "ctx"), "mp"),
        P(("dp", "ctx")),
        P("mp"),
        P(None, "mp"),
    )
    out_specs = P(("dp", "ctx"), "mp")
    return jax.shard_map(
        per_device, mesh=mesh, in_specs=in_specs, out_specs=out_specs, check_vma=False
    )
```

```python
import jax
import jax.numpy as jnp
from jax import lax
from jax.experimental import pallas as pl
from jax.experimental.pallas import tpu as pltpu
from jax.sharding import PartitionSpec as P

HEAD = 128


def features(raw_input):
    return (jax.nn.elu(raw_input.astype(jnp.float32)) + 1.0).astype(jnp.bfloat16)


def _payload_kernel(key_ref, value_ref, seg_ref, out_ref):
    rows, width = key_ref.shape
    heads = width // HEAD
    pieces_per_head = HEAD // 32
    segs = seg_ref[...]
    last = segs[rows - 1 : rows, :]
    first = segs[0:1, :]
    in_final = (segs == last).astype(jnp.float32)
    seg_rows = jnp.where(
        lax.broadcasted_iota(jnp.int32, (8, HEAD), 0) == 0,
        jnp.broadcast_to(last.astype(jnp.float32), (8, HEAD)),
        jnp.broadcast_to(first.astype(jnp.float32), (8, HEAD)),
    )
    for h in range(heads):
        cols = slice(h * HEAD, (h + 1) * HEAD)
        raw = key_ref[:, cols].astype(jnp.float32)
        feat = jnp.where(raw > 0, raw + 1.0, jnp.exp(jnp.minimum(raw, 0.0))).astype(jnp.bfloat16)
        masked = (feat.astype(jnp.float32) * in_final).astype(jnp.bfloat16)
        sums = lax.dot_general(
            value_ref[:, cols], masked, (((0,), (0,)), ((), ())),
            preferred_element_type=jnp.float32,
        )
        for j in range(pieces_per_head):
            piece = h * pieces_per_head + j
            out_ref[piece * 40 : piece * 40 + 32, :] = sums[j * 32 : (j + 1) * 32, :]
            out_ref[piece * 40 + 32 : piece * 40 + 40, :] = seg_rows


def scan_payload(keys, values, segment_ids):
    rows, width = keys.shape
    count = width // 32
    out = pl.pallas_call(
        _payload_kernel,
        out_shape=jax.ShapeDtypeStruct((count * 40, HEAD), jnp.float32),
        in_specs=[pl.BlockSpec(memory_space=pltpu.VMEM)] * 3,
        out_specs=pl.BlockSpec(memory_space=pltpu.VMEM),
    )(keys, values, segment_ids.reshape(rows, 1))
    return out.reshape(count, 40, HEAD)


def carried_in(sent, shape, axis):
    count = lax.axis_size(axis)
    tile = sent.shape[1] - 8
    pieces = lax.all_to_all(sent, axis, 0, 0, tiled=True)
    sums = pieces[:, :tile]
    last_segs = pieces[:, tile, 0]
    first_segs = pieces[:, tile + 1, 0]
    block = jnp.arange(count)
    mask = (block[None, :] < block[:, None]) & (last_segs[None, :] == first_segs[:, None])
    carry = jnp.sum(jnp.where(mask[:, :, None, None], sums[None], 0.0), axis=1)
    return lax.all_to_all(carry, axis, 0, 0, tiled=True).reshape(shape)


def project_gathered(hidden, out_weight, axis):
    count, mine = lax.axis_size(axis), lax.axis_index(axis)
    rows, width = hidden.shape
    half = width // 2
    weight_halves = out_weight.reshape(count, 2, half, out_weight.shape[1])
    ahead = [(j, (j + 1) % count) for j in range(count)]
    behind = [(j, (j - 1) % count) for j in range(count)]

    def rows_of(offset, which):
        return weight_halves[lax.rem(mine + offset + count, count), which]

    def dot(block, weight):
        return jnp.dot(block, weight, preferred_element_type=jnp.float32)

    first, second = hidden[:, :half], hidden[:, half:]
    left_first = lax.ppermute(first, axis, ahead)
    right_second = lax.ppermute(second, axis, behind)
    from_left = lax.ppermute(jnp.concatenate([second, left_first], axis=1), axis, ahead)
    from_right = lax.ppermute(jnp.concatenate([first, right_second], axis=1), axis, behind)
    left_weight = jnp.concatenate([rows_of(-1, 1), rows_of(2, 0)], axis=0)
    right_weight = jnp.concatenate([rows_of(1, 0), rows_of(2, 1)], axis=0)
    total = dot(hidden, out_weight.reshape(count, width, -1)[mine])
    total = total + dot(left_first, rows_of(-1, 0)) + dot(right_second, rows_of(1, 1))
    return total + dot(from_left, left_weight) + dot(from_right, right_weight)


def per_device(queries, keys, values, segment_ids, norm_gain, out_weight):
    rows_here = queries.shape[0]
    width_here = queries.shape[1]
    heads_here = width_here // HEAD
    feat_query = lax.optimization_barrier(features(queries)).reshape(rows_here, heads_here, HEAD)
    feat_key = features(keys).reshape(rows_here, heads_here, HEAD)
    value_heads = values.reshape(rows_here, heads_here, HEAD)
    before_sum = carried_in(
        scan_payload(keys, values, segment_ids), (heads_here, HEAD, HEAD), "ctx"
    )
    position = jnp.arange(rows_here)
    allowed = (position[None, :] <= position[:, None]) & (
        segment_ids[:, None] == segment_ids[None, :]
    )
    scores = jnp.einsum("thd,shd->hts", feat_query, feat_key, preferred_element_type=jnp.float32)
    weights = jnp.where(allowed[None], scores, 0.0).astype(jnp.bfloat16)
    inside = jnp.einsum("hts,she->the", weights, value_heads, preferred_element_type=jnp.float32)
    state_hi = before_sum.astype(jnp.bfloat16)
    state_lo = (before_sum - state_hi.astype(jnp.float32)).astype(jnp.bfloat16)
    carried = jnp.einsum(
        "thd,hed->the", feat_query, state_hi, preferred_element_type=jnp.float32
    ) + jnp.einsum("thd,hed->the", feat_query, state_lo, preferred_element_type=jnp.float32)
    carry_on = (segment_ids == segment_ids[0]).astype(jnp.float32)
    numerator = inside + carry_on[:, None, None] * carried
    normed = numerator * lax.rsqrt(jnp.mean(numerator * numerator, axis=-1, keepdims=True) + 1e-06)
    gain_heads = norm_gain.reshape(heads_here, HEAD)
    hidden = (normed * gain_heads[None]).astype(jnp.bfloat16).reshape(rows_here, width_here)
    return project_gathered(hidden, out_weight, "mp").astype(jnp.bfloat16)


def solution(mesh):
    in_specs = (
        P(("dp", "ctx"), "mp"),
        P(("dp", "ctx"), "mp"),
        P(("dp", "ctx"), "mp"),
        P(("dp", "ctx")),
        P("mp"),
        P(None, "mp"),
    )
    out_specs = P(("dp", "ctx"), "mp")
    return jax.shard_map(
        per_device, mesh=mesh, in_specs=in_specs, out_specs=out_specs, check_vma=False
    )
```

```python
import jax
import jax.numpy as jnp
from jax import lax
from jax.experimental import pallas as pl
from jax.experimental.pallas import tpu as pltpu
from jax.sharding import PartitionSpec as P

HEAD = 128


def features(raw_input):
    return (jax.nn.elu(raw_input.astype(jnp.float32)) + 1.0).astype(jnp.bfloat16)


def _payload_kernel(key_ref, value_ref, seg_ref, out_ref):
    rows, width = key_ref.shape
    heads = width // HEAD
    pieces_per_head = HEAD // 32
    segs = seg_ref[...]
    last = segs[-1:, -1:]
    first = segs[:1, :1]
    final_from = jnp.sum((segs != last).astype(jnp.int32))
    rows_at = lax.broadcasted_iota(jnp.int32, (rows, 1), 0)
    in_final = (rows_at >= final_from).astype(jnp.float32)
    seg_rows = jnp.where(
        lax.broadcasted_iota(jnp.int32, (8, HEAD), 0) == 0,
        jnp.broadcast_to(last.astype(jnp.float32), (8, HEAD)),
        jnp.broadcast_to(first.astype(jnp.float32), (8, HEAD)),
    )
    for h in range(heads):
        cols = slice(h * HEAD, (h + 1) * HEAD)
        raw = key_ref[:, cols].astype(jnp.float32)
        feat = jnp.where(raw > 0, raw + 1.0, jnp.exp(jnp.minimum(raw, 0.0))).astype(jnp.bfloat16)
        masked = (feat.astype(jnp.float32) * in_final).astype(jnp.bfloat16)
        sums = lax.dot_general(
            value_ref[:, cols], masked, (((0,), (0,)), ((), ())),
            preferred_element_type=jnp.float32,
        )
        for j in range(pieces_per_head):
            piece = h * pieces_per_head + j
            out_ref[piece * 40 : piece * 40 + 32, :] = sums[j * 32 : (j + 1) * 32, :]
            out_ref[piece * 40 + 32 : piece * 40 + 40, :] = seg_rows


def scan_payload(keys, values, segment_ids):
    rows, width = keys.shape
    count = width // 32
    out = pl.pallas_call(
        _payload_kernel,
        out_shape=jax.ShapeDtypeStruct((count * 40, HEAD), jnp.float32),
        in_specs=[pl.BlockSpec(memory_space=pltpu.VMEM)] * 3,
        out_specs=pl.BlockSpec(memory_space=pltpu.VMEM),
    )(keys, values, segment_ids.reshape(-1, HEAD))
    return out.reshape(count, 40, HEAD)


def carried_in(sent, shape, axis):
    count = lax.axis_size(axis)
    tile = sent.shape[1] - 8
    pieces = lax.all_to_all(sent, axis, 0, 0, tiled=True)
    sums = pieces[:, :tile]
    last_segs = pieces[:, tile, 0]
    first_segs = pieces[:, tile + 1, 0]
    block = jnp.arange(count)
    mask = (block[None, :] < block[:, None]) & (last_segs[None, :] == first_segs[:, None])
    carry = jnp.sum(jnp.where(mask[:, :, None, None], sums[None], 0.0), axis=1)
    return lax.all_to_all(carry, axis, 0, 0, tiled=True).reshape(shape)


def project_gathered(hidden, out_weight, axis):
    count, mine = lax.axis_size(axis), lax.axis_index(axis)
    rows, width = hidden.shape
    half = width // 2
    weight_halves = out_weight.reshape(count, 2, half, out_weight.shape[1])
    ahead = [(j, (j + 1) % count) for j in range(count)]
    behind = [(j, (j - 1) % count) for j in range(count)]

    def rows_of(offset, which):
        return weight_halves[lax.rem(mine + offset + count, count), which]

    def dot(block, weight):
        return jnp.dot(block, weight, preferred_element_type=jnp.float32)

    first, second = hidden[:, :half], hidden[:, half:]
    left_first = lax.ppermute(first, axis, ahead)
    right_second = lax.ppermute(second, axis, behind)
    from_left = lax.ppermute(jnp.concatenate([second, left_first], axis=1), axis, ahead)
    from_right = lax.ppermute(jnp.concatenate([first, right_second], axis=1), axis, behind)
    left_weight = jnp.concatenate([rows_of(-1, 1), rows_of(2, 0)], axis=0)
    right_weight = jnp.concatenate([rows_of(1, 0), rows_of(2, 1)], axis=0)
    total = dot(hidden, out_weight.reshape(count, width, -1)[mine])
    total = total + dot(left_first, rows_of(-1, 0)) + dot(right_second, rows_of(1, 1))
    return total + dot(from_left, left_weight) + dot(from_right, right_weight)


def per_device(queries, keys, values, segment_ids, norm_gain, out_weight):
    rows_here = queries.shape[0]
    width_here = queries.shape[1]
    heads_here = width_here // HEAD
    feat_query = lax.optimization_barrier(features(queries)).reshape(rows_here, heads_here, HEAD)
    feat_key = features(keys).reshape(rows_here, heads_here, HEAD)
    value_heads = values.reshape(rows_here, heads_here, HEAD)
    before_sum = carried_in(
        scan_payload(keys, values, segment_ids), (heads_here, HEAD, HEAD), "ctx"
    )
    position = jnp.arange(rows_here)
    allowed = (position[None, :] <= position[:, None]) & (
        segment_ids[:, None] == segment_ids[None, :]
    )
    scores = jnp.einsum("thd,shd->hts", feat_query, feat_key, preferred_element_type=jnp.float32)
    weights = jnp.where(allowed[None], scores, 0.0).astype(jnp.bfloat16)
    inside = jnp.einsum("hts,she->the", weights, value_heads, preferred_element_type=jnp.float32)
    state_hi = before_sum.astype(jnp.bfloat16)
    state_lo = (before_sum - state_hi.astype(jnp.float32)).astype(jnp.bfloat16)
    carried = jnp.einsum(
        "thd,hed->the", feat_query, state_hi, preferred_element_type=jnp.float32
    ) + jnp.einsum("thd,hed->the", feat_query, state_lo, preferred_element_type=jnp.float32)
    carry_on = (segment_ids == segment_ids[0]).astype(jnp.float32)
    numerator = inside + carry_on[:, None, None] * carried
    normed = numerator * lax.rsqrt(jnp.mean(numerator * numerator, axis=-1, keepdims=True) + 1e-06)
    gain_heads = norm_gain.reshape(heads_here, HEAD)
    hidden = (normed * gain_heads[None]).astype(jnp.bfloat16).reshape(rows_here, width_here)
    return project_gathered(hidden, out_weight, "mp").astype(jnp.bfloat16)


def solution(mesh):
    in_specs = (
        P(("dp", "ctx"), "mp"),
        P(("dp", "ctx"), "mp"),
        P(("dp", "ctx"), "mp"),
        P(("dp", "ctx")),
        P("mp"),
        P(None, "mp"),
    )
    out_specs = P(("dp", "ctx"), "mp")
    return jax.shard_map(
        per_device, mesh=mesh, in_specs=in_specs, out_specs=out_specs, check_vma=False
    )
```

```python
import jax
import jax.numpy as jnp
from jax import lax
from jax.experimental import pallas as pl
from jax.experimental.pallas import tpu as pltpu
from jax.sharding import PartitionSpec as P

HEAD = 128


def features(raw_input):
    return (jax.nn.elu(raw_input.astype(jnp.float32)) + 1.0).astype(jnp.bfloat16)


def _payload_kernel(key_ref, value_ref, seg_ref, out_ref):
    rows, width = key_ref.shape
    heads = width // HEAD
    pieces_per_head = HEAD // 32
    segs = seg_ref[...]
    last = segs[-1:, -1:]
    first = segs[:1, :1]
    final_from = jnp.sum((segs != last).astype(jnp.int32))
    rows_at = lax.broadcasted_iota(jnp.int32, (rows, 1), 0)
    in_final = (rows_at >= final_from).astype(jnp.float32)
    seg_rows = jnp.where(
        lax.broadcasted_iota(jnp.int32, (8, HEAD), 0) == 0,
        jnp.broadcast_to(last.astype(jnp.float32), (8, HEAD)),
        jnp.broadcast_to(first.astype(jnp.float32), (8, HEAD)),
    )
    for h in range(heads):
        cols = slice(h * HEAD, (h + 1) * HEAD)
        raw = key_ref[:, cols].astype(jnp.float32)
        feat = jnp.where(raw > 0, raw + 1.0, jnp.exp(jnp.minimum(raw, 0.0))).astype(jnp.bfloat16)
        masked = (feat.astype(jnp.float32) * in_final).astype(jnp.bfloat16)
        sums = lax.dot_general(
            value_ref[:, cols], masked, (((0,), (0,)), ((), ())),
            preferred_element_type=jnp.float32,
        )
        for j in range(pieces_per_head):
            piece = h * pieces_per_head + j
            out_ref[piece * 40 : piece * 40 + 32, :] = sums[j * 32 : (j + 1) * 32, :]
            out_ref[piece * 40 + 32 : piece * 40 + 40, :] = seg_rows


def scan_payload(keys, values, segment_ids):
    rows, width = keys.shape
    count = width // 32
    out = pl.pallas_call(
        _payload_kernel,
        out_shape=jax.ShapeDtypeStruct((count * 40, HEAD), jnp.float32),
        in_specs=[pl.BlockSpec(memory_space=pltpu.VMEM)] * 3,
        out_specs=pl.BlockSpec(memory_space=pltpu.VMEM),
    )(keys, values, segment_ids.reshape(-1, HEAD))
    return out.reshape(count, 40, HEAD)


def carried_in(sent, shape, axis):
    count = lax.axis_size(axis)
    tile = sent.shape[1] - 8
    pieces = lax.all_to_all(sent, axis, 0, 0, tiled=True)
    sums = pieces[:, :tile]
    last_segs = pieces[:, tile, 0]
    first_segs = pieces[:, tile + 1, 0]
    block = jnp.arange(count)
    mask = (block[None, :] < block[:, None]) & (last_segs[None, :] == first_segs[:, None])
    carry = jnp.sum(jnp.where(mask[:, :, None, None], sums[None], 0.0), axis=1)
    return lax.all_to_all(carry, axis, 0, 0, tiled=True).reshape(shape)


def project_gathered(hidden, out_weight, axis):
    count, mine = lax.axis_size(axis), lax.axis_index(axis)
    rows, width = hidden.shape
    half = width // 2
    weight_halves = out_weight.reshape(count, 2, half, out_weight.shape[1])
    ahead = [(j, (j + 1) % count) for j in range(count)]
    behind = [(j, (j - 1) % count) for j in range(count)]

    def rows_of(offset, which):
        return weight_halves[lax.rem(mine + offset + count, count), which]

    def dot(block, weight):
        return jnp.dot(block, weight, preferred_element_type=jnp.float32)

    first, second = hidden[:, :half], hidden[:, half:]
    left_first = lax.ppermute(first, axis, ahead)
    right_second = lax.ppermute(second, axis, behind)
    own = dot(hidden, out_weight.reshape(count, width, -1)[mine])
    to_left, to_right, own = lax.optimization_barrier(
        (
            jnp.concatenate([second, left_first], axis=1),
            jnp.concatenate([first, right_second], axis=1),
            own,
        )
    )
    from_left = lax.ppermute(to_left, axis, ahead)
    from_right = lax.ppermute(to_right, axis, behind)
    total = lax.optimization_barrier(own + dot(left_first, rows_of(-1, 0)))
    total = lax.optimization_barrier(total + dot(right_second, rows_of(1, 1)))
    total = total + dot(from_left[:, :half], rows_of(-1, 1)) + dot(from_left[:, half:], rows_of(2, 0))
    return total + dot(from_right[:, :half], rows_of(1, 0)) + dot(from_right[:, half:], rows_of(2, 1))


def per_device(queries, keys, values, segment_ids, norm_gain, out_weight):
    rows_here = queries.shape[0]
    width_here = queries.shape[1]
    heads_here = width_here // HEAD
    feat_query = lax.optimization_barrier(features(queries)).reshape(rows_here, heads_here, HEAD)
    feat_key = features(keys).reshape(rows_here, heads_here, HEAD)
    value_heads = values.reshape(rows_here, heads_here, HEAD)
    before_sum = carried_in(
        scan_payload(keys, values, segment_ids), (heads_here, HEAD, HEAD), "ctx"
    )
    position = jnp.arange(rows_here)
    allowed = (position[None, :] <= position[:, None]) & (
        segment_ids[:, None] == segment_ids[None, :]
    )
    scores = jnp.einsum("thd,shd->hts", feat_query, feat_key, preferred_element_type=jnp.float32)
    weights = jnp.where(allowed[None], scores, 0.0).astype(jnp.bfloat16)
    inside = jnp.einsum("hts,she->the", weights, value_heads, preferred_element_type=jnp.float32)
    state_hi = before_sum.astype(jnp.bfloat16)
    state_lo = (before_sum - state_hi.astype(jnp.float32)).astype(jnp.bfloat16)
    carried = jnp.einsum(
        "thd,hed->the", feat_query, state_hi, preferred_element_type=jnp.float32
    ) + jnp.einsum("thd,hed->the", feat_query, state_lo, preferred_element_type=jnp.float32)
    carry_on = (segment_ids == segment_ids[0]).astype(jnp.float32)
    numerator = inside + carry_on[:, None, None] * carried
    normed = numerator * lax.rsqrt(jnp.mean(numerator * numerator, axis=-1, keepdims=True) + 1e-06)
    gain_heads = norm_gain.reshape(heads_here, HEAD)
    hidden = (normed * gain_heads[None]).astype(jnp.bfloat16).reshape(rows_here, width_here)
    return project_gathered(hidden, out_weight, "mp").astype(jnp.bfloat16)


def solution(mesh):
    in_specs = (
        P(("dp", "ctx"), "mp"),
        P(("dp", "ctx"), "mp"),
        P(("dp", "ctx"), "mp"),
        P(("dp", "ctx")),
        P("mp"),
        P(None, "mp"),
    )
    out_specs = P(("dp", "ctx"), "mp")
    return jax.shard_map(
        per_device, mesh=mesh, in_specs=in_specs, out_specs=out_specs, check_vma=False
    )
```

```python
import jax
import jax.numpy as jnp
from jax import lax
from jax.experimental import pallas as pl
from jax.experimental.pallas import tpu as pltpu
from jax.sharding import PartitionSpec as P

HEAD = 128


def features(raw_input):
    return (jax.nn.elu(raw_input.astype(jnp.float32)) + 1.0).astype(jnp.bfloat16)


def _payload_kernel(key_ref, value_ref, seg_ref, out_ref):
    rows, width = key_ref.shape
    heads = width // HEAD
    pieces_per_head = HEAD // 32
    segs = seg_ref[...]
    last = segs[-1:, -1:]
    first = segs[:1, :1]
    final_from = jnp.sum((segs != last).astype(jnp.int32))
    rows_at = lax.broadcasted_iota(jnp.int32, (rows, 1), 0)
    in_final = (rows_at >= final_from).astype(jnp.float32)
    seg_rows = jnp.where(
        lax.broadcasted_iota(jnp.int32, (8, HEAD), 0) == 0,
        jnp.broadcast_to(last.astype(jnp.float32), (8, HEAD)),
        jnp.broadcast_to(first.astype(jnp.float32), (8, HEAD)),
    )
    for h in range(heads):
        cols = slice(h * HEAD, (h + 1) * HEAD)
        raw = key_ref[:, cols].astype(jnp.float32)
        feat = jnp.where(raw > 0, raw + 1.0, jnp.exp(jnp.minimum(raw, 0.0))).astype(jnp.bfloat16)
        masked = (feat.astype(jnp.float32) * in_final).astype(jnp.bfloat16)
        sums = lax.dot_general(
            value_ref[:, cols], masked, (((0,), (0,)), ((), ())),
            preferred_element_type=jnp.float32,
        )
        for j in range(pieces_per_head):
            piece = h * pieces_per_head + j
            out_ref[piece * 40 : piece * 40 + 32, :] = sums[j * 32 : (j + 1) * 32, :]
            out_ref[piece * 40 + 32 : piece * 40 + 40, :] = seg_rows


def scan_payload(keys, values, segment_ids):
    rows, width = keys.shape
    count = width // 32
    out = pl.pallas_call(
        _payload_kernel,
        out_shape=jax.ShapeDtypeStruct((count * 40, HEAD), jnp.float32),
        in_specs=[pl.BlockSpec(memory_space=pltpu.VMEM)] * 3,
        out_specs=pl.BlockSpec(memory_space=pltpu.VMEM),
    )(keys, values, segment_ids.reshape(-1, HEAD))
    return out.reshape(count, 40, HEAD)


def carried_in(sent, shape, axis):
    count = lax.axis_size(axis)
    tile = sent.shape[1] - 8
    pieces = lax.all_to_all(sent, axis, 0, 0, tiled=True)
    sums = pieces[:, :tile]
    last_segs = pieces[:, tile, 0]
    first_segs = pieces[:, tile + 1, 0]
    block = jnp.arange(count)
    mask = (block[None, :] < block[:, None]) & (last_segs[None, :] == first_segs[:, None])
    carry = jnp.sum(jnp.where(mask[:, :, None, None], sums[None], 0.0), axis=1)
    return lax.all_to_all(carry, axis, 0, 0, tiled=True).reshape(shape)


def project_gathered(hidden, out_weight, axis):
    count, mine = lax.axis_size(axis), lax.axis_index(axis)
    rows, width = hidden.shape
    half = width // 2
    weight_halves = out_weight.reshape(count, 2, half, out_weight.shape[1])
    ahead = [(j, (j + 1) % count) for j in range(count)]
    behind = [(j, (j - 1) % count) for j in range(count)]

    def rows_of(offset, which):
        return weight_halves[lax.rem(mine + offset + count, count), which]

    def dot(block, weight):
        return jnp.dot(block, weight, preferred_element_type=jnp.float32)

    first, second = hidden[:, :half], hidden[:, half:]
    left_first = lax.ppermute(first, axis, ahead)
    right_second = lax.ppermute(second, axis, behind)
    from_left = lax.ppermute(jnp.concatenate([second, left_first], axis=1), axis, ahead)
    from_right = lax.ppermute(jnp.concatenate([first, right_second], axis=1), axis, behind)
    left_weight = jnp.concatenate([rows_of(-1, 1), rows_of(2, 0)], axis=0)
    right_weight = jnp.concatenate([rows_of(1, 0), rows_of(2, 1)], axis=0)
    near = jnp.concatenate([hidden, left_first, right_second], axis=1)
    near_weight = jnp.concatenate(
        [out_weight.reshape(count, width, -1)[mine], rows_of(-1, 0), rows_of(1, 1)], axis=0
    )
    total = dot(near, near_weight)
    return total + dot(from_left, left_weight) + dot(from_right, right_weight)


def per_device(queries, keys, values, segment_ids, norm_gain, out_weight):
    rows_here = queries.shape[0]
    width_here = queries.shape[1]
    heads_here = width_here // HEAD
    feat_query = lax.optimization_barrier(features(queries)).reshape(rows_here, heads_here, HEAD)
    feat_key = features(keys).reshape(rows_here, heads_here, HEAD)
    value_heads = values.reshape(rows_here, heads_here, HEAD)
    before_sum = carried_in(
        scan_payload(keys, values, segment_ids), (heads_here, HEAD, HEAD), "ctx"
    )
    position = jnp.arange(rows_here)
    allowed = (position[None, :] <= position[:, None]) & (
        segment_ids[:, None] == segment_ids[None, :]
    )
    scores = jnp.einsum("thd,shd->hts", feat_query, feat_key, preferred_element_type=jnp.float32)
    weights = jnp.where(allowed[None], scores, 0.0).astype(jnp.bfloat16)
    inside = jnp.einsum("hts,she->the", weights, value_heads, preferred_element_type=jnp.float32)
    state_hi = before_sum.astype(jnp.bfloat16)
    state_lo = (before_sum - state_hi.astype(jnp.float32)).astype(jnp.bfloat16)
    carried = jnp.einsum(
        "thd,hed->the", feat_query, state_hi, preferred_element_type=jnp.float32
    ) + jnp.einsum("thd,hed->the", feat_query, state_lo, preferred_element_type=jnp.float32)
    carry_on = (segment_ids == segment_ids[0]).astype(jnp.float32)
    numerator = inside + carry_on[:, None, None] * carried
    normed = numerator * lax.rsqrt(jnp.mean(numerator * numerator, axis=-1, keepdims=True) + 1e-06)
    gain_heads = norm_gain.reshape(heads_here, HEAD)
    hidden = (normed * gain_heads[None]).astype(jnp.bfloat16).reshape(rows_here, width_here)
    return project_gathered(hidden, out_weight, "mp").astype(jnp.bfloat16)


def solution(mesh):
    in_specs = (
        P(("dp", "ctx"), "mp"),
        P(("dp", "ctx"), "mp"),
        P(("dp", "ctx"), "mp"),
        P(("dp", "ctx")),
        P("mp"),
        P(None, "mp"),
    )
    out_specs = P(("dp", "ctx"), "mp")
    return jax.shard_map(
        per_device, mesh=mesh, in_specs=in_specs, out_specs=out_specs, check_vma=False
    )
```

```python
import jax
import jax.numpy as jnp
from jax import lax
from jax.experimental import pallas as pl
from jax.experimental.pallas import tpu as pltpu
from jax.sharding import PartitionSpec as P

HEAD = 128


def features(raw_input):
    return (jax.nn.elu(raw_input.astype(jnp.float32)) + 1.0).astype(jnp.bfloat16)


def _payload_kernel(key_ref, value_ref, seg_ref, out_ref):
    rows, width = key_ref.shape
    heads = width // HEAD
    pieces_per_head = HEAD // 32
    segs = seg_ref[...]
    last = segs[-1:, -1:]
    first = segs[:1, :1]
    final_from = jnp.sum((segs != last).astype(jnp.int32))
    rows_at = lax.broadcasted_iota(jnp.int32, (rows, 1), 0)
    in_final = (rows_at >= final_from).astype(jnp.float32)
    seg_rows = jnp.where(
        lax.broadcasted_iota(jnp.int32, (8, HEAD), 0) == 0,
        jnp.broadcast_to(last.astype(jnp.float32), (8, HEAD)),
        jnp.broadcast_to(first.astype(jnp.float32), (8, HEAD)),
    )
    for h in range(heads):
        cols = slice(h * HEAD, (h + 1) * HEAD)
        raw = key_ref[:, cols].astype(jnp.float32)
        feat = jnp.where(raw > 0, raw + 1.0, jnp.exp(jnp.minimum(raw, 0.0))).astype(jnp.bfloat16)
        masked = (feat.astype(jnp.float32) * in_final).astype(jnp.bfloat16)
        sums = lax.dot_general(
            value_ref[:, cols], masked, (((0,), (0,)), ((), ())),
            preferred_element_type=jnp.float32,
        )
        for j in range(pieces_per_head):
            piece = h * pieces_per_head + j
            out_ref[piece * 40 : piece * 40 + 32, :] = sums[j * 32 : (j + 1) * 32, :]
            out_ref[piece * 40 + 32 : piece * 40 + 40, :] = seg_rows


def scan_payload(keys, values, segment_ids):
    rows, width = keys.shape
    count = width // 32
    out = pl.pallas_call(
        _payload_kernel,
        out_shape=jax.ShapeDtypeStruct((count * 40, HEAD), jnp.float32),
        in_specs=[pl.BlockSpec(memory_space=pltpu.VMEM)] * 3,
        out_specs=pl.BlockSpec(memory_space=pltpu.VMEM),
    )(keys, values, segment_ids.reshape(-1, HEAD))
    return out.reshape(count, 40, HEAD)


def carried_in(sent, shape, axis):
    count = lax.axis_size(axis)
    tile = sent.shape[1] - 8
    pieces = lax.all_to_all(sent, axis, 0, 0, tiled=True)
    sums = pieces[:, :tile]
    last_segs = pieces[:, tile, 0]
    first_segs = pieces[:, tile + 1, 0]
    block = jnp.arange(count)
    mask = (block[None, :] < block[:, None]) & (last_segs[None, :] == first_segs[:, None])
    carry = jnp.dot(
        mask.astype(jnp.float32),
        sums.reshape(count, -1),
        precision=lax.Precision.HIGHEST,
        preferred_element_type=jnp.float32,
    ).reshape(sums.shape)
    return lax.all_to_all(carry, axis, 0, 0, tiled=True).reshape(shape)


def project_gathered(hidden, out_weight, axis):
    count, mine = lax.axis_size(axis), lax.axis_index(axis)
    rows, width = hidden.shape
    half = width // 2
    weight_halves = out_weight.reshape(count, 2, half, out_weight.shape[1])
    ahead = [(j, (j + 1) % count) for j in range(count)]
    behind = [(j, (j - 1) % count) for j in range(count)]

    def rows_of(offset, which):
        return weight_halves[lax.rem(mine + offset + count, count), which]

    def dot(block, weight):
        return jnp.dot(block, weight, preferred_element_type=jnp.float32)

    first, second = hidden[:, :half], hidden[:, half:]
    left_first = lax.ppermute(first, axis, ahead)
    right_second = lax.ppermute(second, axis, behind)
    from_left = lax.ppermute(jnp.concatenate([second, left_first], axis=1), axis, ahead)
    from_right = lax.ppermute(jnp.concatenate([first, right_second], axis=1), axis, behind)
    left_weight = jnp.concatenate([rows_of(-1, 1), rows_of(2, 0)], axis=0)
    right_weight = jnp.concatenate([rows_of(1, 0), rows_of(2, 1)], axis=0)
    total = dot(hidden, out_weight.reshape(count, width, -1)[mine])
    total = total + dot(left_first, rows_of(-1, 0)) + dot(right_second, rows_of(1, 1))
    return total + dot(from_left, left_weight) + dot(from_right, right_weight)


def per_device(queries, keys, values, segment_ids, norm_gain, out_weight):
    rows_here = queries.shape[0]
    width_here = queries.shape[1]
    heads_here = width_here // HEAD
    feat_query = lax.optimization_barrier(features(queries)).reshape(rows_here, heads_here, HEAD)
    feat_key = features(keys).reshape(rows_here, heads_here, HEAD)
    value_heads = values.reshape(rows_here, heads_here, HEAD)
    before_sum = carried_in(
        scan_payload(keys, values, segment_ids), (heads_here, HEAD, HEAD), "ctx"
    )
    position = jnp.arange(rows_here)
    allowed = (position[None, :] <= position[:, None]) & (
        segment_ids[:, None] == segment_ids[None, :]
    )
    scores = jnp.einsum("thd,shd->hts", feat_query, feat_key, preferred_element_type=jnp.float32)
    weights = jnp.where(allowed[None], scores, 0.0).astype(jnp.bfloat16)
    inside = jnp.einsum("hts,she->the", weights, value_heads, preferred_element_type=jnp.float32)
    state_hi = before_sum.astype(jnp.bfloat16)
    state_lo = (before_sum - state_hi.astype(jnp.float32)).astype(jnp.bfloat16)
    carried = jnp.einsum(
        "thd,hed->the", feat_query, state_hi, preferred_element_type=jnp.float32
    ) + jnp.einsum("thd,hed->the", feat_query, state_lo, preferred_element_type=jnp.float32)
    carry_on = (segment_ids == segment_ids[0]).astype(jnp.float32)
    numerator = inside + carry_on[:, None, None] * carried
    normed = numerator * lax.rsqrt(jnp.mean(numerator * numerator, axis=-1, keepdims=True) + 1e-06)
    gain_heads = norm_gain.reshape(heads_here, HEAD)
    hidden = (normed * gain_heads[None]).astype(jnp.bfloat16).reshape(rows_here, width_here)
    return project_gathered(hidden, out_weight, "mp").astype(jnp.bfloat16)


def solution(mesh):
    in_specs = (
        P(("dp", "ctx"), "mp"),
        P(("dp", "ctx"), "mp"),
        P(("dp", "ctx"), "mp"),
        P(("dp", "ctx")),
        P("mp"),
        P(None, "mp"),
    )
    out_specs = P(("dp", "ctx"), "mp")
    return jax.shard_map(
        per_device, mesh=mesh, in_specs=in_specs, out_specs=out_specs, check_vma=False
    )
```

```python
import jax
import jax.numpy as jnp
from jax import lax
from jax.experimental import pallas as pl
from jax.experimental.pallas import tpu as pltpu
from jax.sharding import PartitionSpec as P

HEAD = 128


def features(raw_input):
    return (jax.nn.elu(raw_input.astype(jnp.float32)) + 1.0).astype(jnp.bfloat16)


def _payload_kernel(key_ref, value_ref, seg_ref, out_ref):
    rows = key_ref.shape[0]
    pieces_per_head = HEAD // 32
    segs = seg_ref[...]
    last = segs[-1:, -1:]
    first = segs[:1, :1]
    final_from = jnp.sum((segs != last).astype(jnp.int32))
    rows_at = lax.broadcasted_iota(jnp.int32, (rows, 1), 0)
    in_final = (rows_at >= final_from).astype(jnp.float32)
    seg_rows = jnp.where(
        lax.broadcasted_iota(jnp.int32, (8, HEAD), 0) == 0,
        jnp.broadcast_to(last.astype(jnp.float32), (8, HEAD)),
        jnp.broadcast_to(first.astype(jnp.float32), (8, HEAD)),
    )
    raw = key_ref[...].astype(jnp.float32)
    feat = jnp.where(raw > 0, raw + 1.0, jnp.exp(jnp.minimum(raw, 0.0))).astype(jnp.bfloat16)
    masked = (feat.astype(jnp.float32) * in_final).astype(jnp.bfloat16)
    sums = lax.dot_general(
        value_ref[...], masked, (((0,), (0,)), ((), ())),
        preferred_element_type=jnp.float32,
    )
    for j in range(pieces_per_head):
        out_ref[j * 40 : j * 40 + 32, :] = sums[j * 32 : (j + 1) * 32, :]
        out_ref[j * 40 + 32 : j * 40 + 40, :] = seg_rows


def scan_payload(keys, values, segment_ids):
    rows, width = keys.shape
    count = width // 32
    heads = width // HEAD
    seg_tiles = segment_ids.reshape(-1, HEAD)
    out = pl.pallas_call(
        _payload_kernel,
        out_shape=jax.ShapeDtypeStruct((count * 40, HEAD), jnp.float32),
        grid=(heads,),
        in_specs=[
            pl.BlockSpec((rows, HEAD), lambda h: (0, h)),
            pl.BlockSpec((rows, HEAD), lambda h: (0, h)),
            pl.BlockSpec(seg_tiles.shape, lambda h: (0, 0)),
        ],
        out_specs=pl.BlockSpec((count // heads * 40, HEAD), lambda h: (h, 0)),
    )(keys, values, seg_tiles)
    return out.reshape(count, 40, HEAD)


def carried_in(sent, shape, axis):
    count = lax.axis_size(axis)
    tile = sent.shape[1] - 8
    pieces = lax.all_to_all(sent, axis, 0, 0, tiled=True)
    sums = pieces[:, :tile]
    last_segs = pieces[:, tile, 0]
    first_segs = pieces[:, tile + 1, 0]
    block = jnp.arange(count)
    mask = (block[None, :] < block[:, None]) & (last_segs[None, :] == first_segs[:, None])
    carry = jnp.sum(jnp.where(mask[:, :, None, None], sums[None], 0.0), axis=1)
    return lax.all_to_all(carry, axis, 0, 0, tiled=True).reshape(shape)


def project_gathered(hidden, out_weight, axis):
    count, mine = lax.axis_size(axis), lax.axis_index(axis)
    rows, width = hidden.shape
    half = width // 2
    weight_halves = out_weight.reshape(count, 2, half, out_weight.shape[1])
    ahead = [(j, (j + 1) % count) for j in range(count)]
    behind = [(j, (j - 1) % count) for j in range(count)]

    def rows_of(offset, which):
        return weight_halves[lax.rem(mine + offset + count, count), which]

    def dot(block, weight):
        return jnp.dot(block, weight, preferred_element_type=jnp.float32)

    first, second = hidden[:, :half], hidden[:, half:]
    left_first = lax.ppermute(first, axis, ahead)
    right_second = lax.ppermute(second, axis, behind)
    from_left = lax.ppermute(jnp.concatenate([second, left_first], axis=1), axis, ahead)
    from_right = lax.ppermute(jnp.concatenate([first, right_second], axis=1), axis, behind)
    left_weight = jnp.concatenate([rows_of(-1, 1), rows_of(2, 0)], axis=0)
    right_weight = jnp.concatenate([rows_of(1, 0), rows_of(2, 1)], axis=0)
    total = dot(hidden, out_weight.reshape(count, width, -1)[mine])
    total = total + dot(left_first, rows_of(-1, 0)) + dot(right_second, rows_of(1, 1))
    return total + dot(from_left, left_weight) + dot(from_right, right_weight)


def per_device(queries, keys, values, segment_ids, norm_gain, out_weight):
    rows_here = queries.shape[0]
    width_here = queries.shape[1]
    heads_here = width_here // HEAD
    feat_query = lax.optimization_barrier(features(queries)).reshape(rows_here, heads_here, HEAD)
    feat_key = features(keys).reshape(rows_here, heads_here, HEAD)
    value_heads = values.reshape(rows_here, heads_here, HEAD)
    before_sum = carried_in(
        scan_payload(keys, values, segment_ids), (heads_here, HEAD, HEAD), "ctx"
    )
    position = jnp.arange(rows_here)
    allowed = (position[None, :] <= position[:, None]) & (
        segment_ids[:, None] == segment_ids[None, :]
    )
    scores = jnp.einsum("thd,shd->hts", feat_query, feat_key, preferred_element_type=jnp.float32)
    weights = jnp.where(allowed[None], scores, 0.0).astype(jnp.bfloat16)
    inside = jnp.einsum("hts,she->the", weights, value_heads, preferred_element_type=jnp.float32)
    state_hi = before_sum.astype(jnp.bfloat16)
    state_lo = (before_sum - state_hi.astype(jnp.float32)).astype(jnp.bfloat16)
    carried = jnp.einsum(
        "thd,hed->the", feat_query, state_hi, preferred_element_type=jnp.float32
    ) + jnp.einsum("thd,hed->the", feat_query, state_lo, preferred_element_type=jnp.float32)
    carry_on = (segment_ids == segment_ids[0]).astype(jnp.float32)
    numerator = inside + carry_on[:, None, None] * carried
    normed = numerator * lax.rsqrt(jnp.mean(numerator * numerator, axis=-1, keepdims=True) + 1e-06)
    gain_heads = norm_gain.reshape(heads_here, HEAD)
    hidden = (normed * gain_heads[None]).astype(jnp.bfloat16).reshape(rows_here, width_here)
    return project_gathered(hidden, out_weight, "mp").astype(jnp.bfloat16)


def solution(mesh):
    in_specs = (
        P(("dp", "ctx"), "mp"),
        P(("dp", "ctx"), "mp"),
        P(("dp", "ctx"), "mp"),
        P(("dp", "ctx")),
        P("mp"),
        P(None, "mp"),
    )
    out_specs = P(("dp", "ctx"), "mp")
    return jax.shard_map(
        per_device, mesh=mesh, in_specs=in_specs, out_specs=out_specs, check_vma=False
    )
```

```python
import jax
import jax.numpy as jnp
from jax import lax
from jax.experimental import pallas as pl
from jax.experimental.pallas import tpu as pltpu
from jax.sharding import PartitionSpec as P

HEAD = 128


def features(raw_input):
    return (jax.nn.elu(raw_input.astype(jnp.float32)) + 1.0).astype(jnp.bfloat16)


def _payload_kernel(key_ref, value_ref, seg_ref, out_ref):
    rows, width = key_ref.shape
    heads = width // HEAD
    pieces_per_head = HEAD // 32
    segs = seg_ref[...]
    last = segs[-1:, -1:]
    first = segs[:1, :1]
    final_from = jnp.sum((segs != last).astype(jnp.int32))
    rows_at = lax.broadcasted_iota(jnp.int32, (rows, 1), 0)
    in_final = rows_at >= final_from
    seg_rows = jnp.where(
        lax.broadcasted_iota(jnp.int32, (8, HEAD), 0) == 0,
        jnp.broadcast_to(last.astype(jnp.float32), (8, HEAD)),
        jnp.broadcast_to(first.astype(jnp.float32), (8, HEAD)),
    )
    for h in range(heads):
        cols = slice(h * HEAD, (h + 1) * HEAD)
        raw = key_ref[:, cols].astype(jnp.float32)
        feat = jnp.where(raw > 0, raw + 1.0, jnp.exp(jnp.minimum(raw, 0.0))).astype(jnp.bfloat16)
        masked = jnp.where(in_final, feat, jnp.zeros_like(feat))
        sums = lax.dot_general(
            value_ref[:, cols], masked, (((0,), (0,)), ((), ())),
            preferred_element_type=jnp.float32,
        )
        for j in range(pieces_per_head):
            piece = h * pieces_per_head + j
            out_ref[piece * 40 : piece * 40 + 32, :] = sums[j * 32 : (j + 1) * 32, :]
            out_ref[piece * 40 + 32 : piece * 40 + 40, :] = seg_rows


def scan_payload(keys, values, segment_ids):
    rows, width = keys.shape
    count = width // 32
    out = pl.pallas_call(
        _payload_kernel,
        out_shape=jax.ShapeDtypeStruct((count * 40, HEAD), jnp.float32),
        in_specs=[pl.BlockSpec(memory_space=pltpu.VMEM)] * 3,
        out_specs=pl.BlockSpec(memory_space=pltpu.VMEM),
    )(keys, values, segment_ids.reshape(-1, HEAD))
    return out.reshape(count, 40, HEAD)


def carried_in(sent, shape, axis):
    count = lax.axis_size(axis)
    tile = sent.shape[1] - 8
    pieces = lax.all_to_all(sent, axis, 0, 0, tiled=True)
    sums = pieces[:, :tile]
    last_segs = pieces[:, tile, 0]
    first_segs = pieces[:, tile + 1, 0]
    block = jnp.arange(count)
    mask = (block[None, :] < block[:, None]) & (last_segs[None, :] == first_segs[:, None])
    carry = jnp.dot(
        mask.astype(jnp.float32),
        sums.reshape(count, -1),
        precision=lax.Precision.HIGHEST,
        preferred_element_type=jnp.float32,
    ).reshape(sums.shape)
    return lax.all_to_all(carry, axis, 0, 0, tiled=True).reshape(shape)


def project_gathered(hidden, out_weight, axis):
    count, mine = lax.axis_size(axis), lax.axis_index(axis)
    rows, width = hidden.shape
    half = width // 2
    weight_halves = out_weight.reshape(count, 2, half, out_weight.shape[1])
    ahead = [(j, (j + 1) % count) for j in range(count)]
    behind = [(j, (j - 1) % count) for j in range(count)]

    def rows_of(offset, which):
        return weight_halves[lax.rem(mine + offset + count, count), which]

    def dot(block, weight):
        return jnp.dot(block, weight, preferred_element_type=jnp.float32)

    first, second = hidden[:, :half], hidden[:, half:]
    left_first = lax.ppermute(first, axis, ahead)
    right_second = lax.ppermute(second, axis, behind)
    from_left = lax.ppermute(jnp.concatenate([second, left_first], axis=1), axis, ahead)
    from_right = lax.ppermute(jnp.concatenate([first, right_second], axis=1), axis, behind)
    left_weight = jnp.concatenate([rows_of(-1, 1), rows_of(2, 0)], axis=0)
    right_weight = jnp.concatenate([rows_of(1, 0), rows_of(2, 1)], axis=0)
    total = dot(hidden, out_weight.reshape(count, width, -1)[mine])
    total = total + dot(left_first, rows_of(-1, 0)) + dot(right_second, rows_of(1, 1))
    return total + dot(from_left, left_weight) + dot(from_right, right_weight)


def per_device(queries, keys, values, segment_ids, norm_gain, out_weight):
    rows_here = queries.shape[0]
    width_here = queries.shape[1]
    heads_here = width_here // HEAD
    feat_query = lax.optimization_barrier(features(queries)).reshape(rows_here, heads_here, HEAD)
    feat_key = features(keys).reshape(rows_here, heads_here, HEAD)
    value_heads = values.reshape(rows_here, heads_here, HEAD)
    before_sum = carried_in(
        scan_payload(keys, values, segment_ids), (heads_here, HEAD, HEAD), "ctx"
    )
    position = jnp.arange(rows_here)
    allowed = (position[None, :] <= position[:, None]) & (
        segment_ids[:, None] == segment_ids[None, :]
    )
    scores = jnp.einsum("thd,shd->hts", feat_query, feat_key, preferred_element_type=jnp.float32)
    weights = jnp.where(allowed[None], scores, 0.0).astype(jnp.bfloat16)
    inside = jnp.einsum("hts,she->the", weights, value_heads, preferred_element_type=jnp.float32)
    state_hi = before_sum.astype(jnp.bfloat16)
    state_lo = (before_sum - state_hi.astype(jnp.float32)).astype(jnp.bfloat16)
    carried = jnp.einsum(
        "thd,hed->the", feat_query, state_hi, preferred_element_type=jnp.float32
    ) + jnp.einsum("thd,hed->the", feat_query, state_lo, preferred_element_type=jnp.float32)
    carry_on = (segment_ids == segment_ids[0]).astype(jnp.float32)
    numerator = inside + carry_on[:, None, None] * carried
    normed = numerator * lax.rsqrt(jnp.mean(numerator * numerator, axis=-1, keepdims=True) + 1e-06)
    gain_heads = norm_gain.reshape(heads_here, HEAD)
    hidden = (normed * gain_heads[None]).astype(jnp.bfloat16).reshape(rows_here, width_here)
    return project_gathered(hidden, out_weight, "mp").astype(jnp.bfloat16)


def solution(mesh):
    in_specs = (
        P(("dp", "ctx"), "mp"),
        P(("dp", "ctx"), "mp"),
        P(("dp", "ctx"), "mp"),
        P(("dp", "ctx")),
        P("mp"),
        P(None, "mp"),
    )
    out_specs = P(("dp", "ctx"), "mp")
    return jax.shard_map(
        per_device, mesh=mesh, in_specs=in_specs, out_specs=out_specs, check_vma=False
    )
```

```python
import jax
import jax.numpy as jnp
from jax import lax
from jax.experimental import pallas as pl
from jax.experimental.pallas import tpu as pltpu
from jax.sharding import PartitionSpec as P

HEAD = 128


def features(raw_input):
    return (jax.nn.elu(raw_input.astype(jnp.float32)) + 1.0).astype(jnp.bfloat16)


def _payload_kernel(key_ref, value_ref, seg_ref, out_ref):
    rows, width = key_ref.shape
    heads = width // HEAD
    pieces_per_head = HEAD // 32
    segs = seg_ref[...]
    last = segs[-1:, -1:]
    first = segs[:1, :1]
    final_from = jnp.sum((segs != last).astype(jnp.int32))
    rows_at = lax.broadcasted_iota(jnp.int32, (rows, 1), 0)
    in_final = (rows_at >= final_from).astype(jnp.float32)
    seg_rows = jnp.where(
        lax.broadcasted_iota(jnp.int32, (8, HEAD), 0) == 0,
        jnp.broadcast_to(last.astype(jnp.float32), (8, HEAD)),
        jnp.broadcast_to(first.astype(jnp.float32), (8, HEAD)),
    )
    for h in range(heads):
        cols = slice(h * HEAD, (h + 1) * HEAD)
        raw = key_ref[:, cols].astype(jnp.float32)
        feat = jnp.where(raw > 0, raw + 1.0, jnp.exp(jnp.minimum(raw, 0.0))).astype(jnp.bfloat16)
        masked = (feat.astype(jnp.float32) * in_final).astype(jnp.bfloat16)
        sums = lax.dot_general(
            value_ref[:, cols], masked, (((0,), (0,)), ((), ())),
            preferred_element_type=jnp.float32,
        )
        for j in range(pieces_per_head):
            piece = h * pieces_per_head + j
            out_ref[piece * 40 : piece * 40 + 32, :] = sums[j * 32 : (j + 1) * 32, :]
            out_ref[piece * 40 + 32 : piece * 40 + 40, :] = seg_rows


def scan_payload(keys, values, segment_ids):
    rows, width = keys.shape
    count = width // 32
    out = pl.pallas_call(
        _payload_kernel,
        out_shape=jax.ShapeDtypeStruct((count * 40, HEAD), jnp.float32),
        in_specs=[pl.BlockSpec(memory_space=pltpu.VMEM)] * 3,
        out_specs=pl.BlockSpec(memory_space=pltpu.VMEM),
    )(keys, values, segment_ids.reshape(-1, HEAD))
    return out.reshape(count, 40, HEAD)


def carried_in(sent, shape, axis):
    count = lax.axis_size(axis)
    tile = sent.shape[1] - 8
    pieces = lax.all_to_all(sent, axis, 0, 0, tiled=True)
    sums = pieces[:, :tile]
    last_segs = pieces[:, tile, 0]
    first_segs = pieces[:, tile + 1, 0]
    block = jnp.arange(count)
    mask = (block[None, :] < block[:, None]) & (last_segs[None, :] == first_segs[:, None])
    carry = jnp.sum(jnp.where(mask[:, :, None, None], sums[None], 0.0), axis=1)
    return lax.all_to_all(carry, axis, 0, 0, tiled=True).reshape(shape)


def project_gathered(hidden, out_weight, axis):
    count, mine = lax.axis_size(axis), lax.axis_index(axis)
    rows, width = hidden.shape
    half = width // 2
    weight_halves = out_weight.reshape(count, 2, half, out_weight.shape[1])
    ahead = [(j, (j + 1) % count) for j in range(count)]
    behind = [(j, (j - 1) % count) for j in range(count)]

    def rows_of(offset, which):
        return weight_halves[lax.rem(mine + offset + count, count), which]

    def dot(block, weight):
        return jnp.dot(block, weight, preferred_element_type=jnp.float32)

    first, second = hidden[:, :half], hidden[:, half:]
    left_first = lax.ppermute(first, axis, ahead)
    right_second = lax.ppermute(second, axis, behind)
    from_left = lax.ppermute(jnp.concatenate([second, left_first], axis=1), axis, ahead)
    from_right = lax.ppermute(jnp.concatenate([first, right_second], axis=1), axis, behind)
    left_weight = jnp.concatenate([rows_of(-1, 1), rows_of(2, 0)], axis=0)
    right_weight = jnp.concatenate([rows_of(1, 0), rows_of(2, 1)], axis=0)
    total = dot(hidden, out_weight.reshape(count, width, -1)[mine])
    total = total + dot(left_first, rows_of(-1, 0)) + dot(right_second, rows_of(1, 1))
    far_weight = jnp.concatenate([left_weight, right_weight], axis=0)
    return total + dot(jnp.concatenate([from_left, from_right], axis=1), far_weight)


def per_device(queries, keys, values, segment_ids, norm_gain, out_weight):
    rows_here = queries.shape[0]
    width_here = queries.shape[1]
    heads_here = width_here // HEAD
    feat_query = lax.optimization_barrier(features(queries)).reshape(rows_here, heads_here, HEAD)
    feat_key = features(keys).reshape(rows_here, heads_here, HEAD)
    value_heads = values.reshape(rows_here, heads_here, HEAD)
    before_sum = carried_in(
        scan_payload(keys, values, segment_ids), (heads_here, HEAD, HEAD), "ctx"
    )
    position = jnp.arange(rows_here)
    allowed = (position[None, :] <= position[:, None]) & (
        segment_ids[:, None] == segment_ids[None, :]
    )
    scores = jnp.einsum("thd,shd->hts", feat_query, feat_key, preferred_element_type=jnp.float32)
    weights = jnp.where(allowed[None], scores, 0.0).astype(jnp.bfloat16)
    inside = jnp.einsum("hts,she->the", weights, value_heads, preferred_element_type=jnp.float32)
    state_hi = before_sum.astype(jnp.bfloat16)
    state_lo = (before_sum - state_hi.astype(jnp.float32)).astype(jnp.bfloat16)
    carried = jnp.einsum(
        "thd,hed->the", feat_query, state_hi, preferred_element_type=jnp.float32
    ) + jnp.einsum("thd,hed->the", feat_query, state_lo, preferred_element_type=jnp.float32)
    carry_on = (segment_ids == segment_ids[0]).astype(jnp.float32)
    numerator = inside + carry_on[:, None, None] * carried
    normed = numerator * lax.rsqrt(jnp.mean(numerator * numerator, axis=-1, keepdims=True) + 1e-06)
    gain_heads = norm_gain.reshape(heads_here, HEAD)
    hidden = (normed * gain_heads[None]).astype(jnp.bfloat16).reshape(rows_here, width_here)
    return project_gathered(hidden, out_weight, "mp").astype(jnp.bfloat16)


def solution(mesh):
    in_specs = (
        P(("dp", "ctx"), "mp"),
        P(("dp", "ctx"), "mp"),
        P(("dp", "ctx"), "mp"),
        P(("dp", "ctx")),
        P("mp"),
        P(None, "mp"),
    )
    out_specs = P(("dp", "ctx"), "mp")
    return jax.shard_map(
        per_device, mesh=mesh, in_specs=in_specs, out_specs=out_specs, check_vma=False
    )
```

```python
import jax
import jax.numpy as jnp
from jax import lax
from jax.experimental import pallas as pl
from jax.experimental.pallas import tpu as pltpu
from jax.sharding import PartitionSpec as P

HEAD = 128


def features(raw_input):
    return (jax.nn.elu(raw_input.astype(jnp.float32)) + 1.0).astype(jnp.bfloat16)


def _payload_kernel(key_ref, value_ref, seg_ref, out_ref):
    rows, width = key_ref.shape
    heads = width // HEAD
    pieces_per_head = HEAD // 32
    segs = seg_ref[...]
    last = segs[-1:, -1:]
    first = segs[:1, :1]
    final_from = jnp.sum((segs != last).astype(jnp.int32))
    rows_at = lax.broadcasted_iota(jnp.int32, (rows, 1), 0)
    in_final = rows_at >= final_from
    seg_rows = jnp.where(
        lax.broadcasted_iota(jnp.int32, (8, HEAD), 0) == 0,
        jnp.broadcast_to(last.astype(jnp.float32), (8, HEAD)),
        jnp.broadcast_to(first.astype(jnp.float32), (8, HEAD)),
    )
    for h in range(heads):
        cols = slice(h * HEAD, (h + 1) * HEAD)
        raw = key_ref[:, cols].astype(jnp.float32)
        feat = jnp.where(raw > 0, raw + 1.0, jnp.exp(jnp.minimum(raw, 0.0))).astype(jnp.bfloat16)
        masked = jnp.where(in_final, feat, jnp.zeros_like(feat))
        sums = lax.dot_general(
            value_ref[:, cols], masked, (((0,), (0,)), ((), ())),
            preferred_element_type=jnp.float32,
        )
        for j in range(pieces_per_head):
            piece = h * pieces_per_head + j
            out_ref[piece * 40 : piece * 40 + 32, :] = sums[j * 32 : (j + 1) * 32, :]
            out_ref[piece * 40 + 32 : piece * 40 + 40, :] = seg_rows


def scan_payload(keys, values, segment_ids):
    rows, width = keys.shape
    count = width // 32
    out = pl.pallas_call(
        _payload_kernel,
        out_shape=jax.ShapeDtypeStruct((count * 40, HEAD), jnp.float32),
        in_specs=[pl.BlockSpec(memory_space=pltpu.VMEM)] * 3,
        out_specs=pl.BlockSpec(memory_space=pltpu.VMEM),
    )(keys, values, segment_ids.reshape(-1, HEAD))
    return out.reshape(count, 40, HEAD)


def carried_in(sent, shape, axis):
    count = lax.axis_size(axis)
    tile = sent.shape[1] - 8
    pieces = lax.all_to_all(sent, axis, 0, 0, tiled=True)
    sums = pieces[:, :tile]
    last_segs = pieces[:, tile, 0]
    first_segs = pieces[:, tile + 1, 0]
    block = jnp.arange(count)
    mask = (block[None, :] < block[:, None]) & (last_segs[None, :] == first_segs[:, None])
    carry = jnp.sum(jnp.where(mask[:, :, None, None], sums[None], 0.0), axis=1)
    return lax.all_to_all(carry, axis, 0, 0, tiled=True).reshape(shape)


def project_gathered(hidden, out_weight, axis):
    count, mine = lax.axis_size(axis), lax.axis_index(axis)
    rows, width = hidden.shape
    half = width // 2
    weight_halves = out_weight.reshape(count, 2, half, out_weight.shape[1])
    ahead = [(j, (j + 1) % count) for j in range(count)]
    behind = [(j, (j - 1) % count) for j in range(count)]

    def rows_of(offset, which):
        return weight_halves[lax.rem(mine + offset + count, count), which]

    def dot(block, weight):
        return jnp.dot(block, weight, preferred_element_type=jnp.float32)

    first, second = hidden[:, :half], hidden[:, half:]
    left_first = lax.ppermute(first, axis, ahead)
    right_second = lax.ppermute(second, axis, behind)
    from_left = lax.ppermute(jnp.concatenate([second, left_first], axis=1), axis, ahead)
    from_right = lax.ppermute(jnp.concatenate([first, right_second], axis=1), axis, behind)
    left_weight = jnp.concatenate([rows_of(-1, 1), rows_of(2, 0)], axis=0)
    right_weight = jnp.concatenate([rows_of(1, 0), rows_of(2, 1)], axis=0)
    total = dot(hidden, out_weight.reshape(count, width, -1)[mine])
    total = total + dot(left_first, rows_of(-1, 0)) + dot(right_second, rows_of(1, 1))
    return total + dot(from_left, left_weight) + dot(from_right, right_weight)


def per_device(queries, keys, values, segment_ids, norm_gain, out_weight):
    rows_here = queries.shape[0]
    width_here = queries.shape[1]
    heads_here = width_here // HEAD
    feat_query = lax.optimization_barrier(features(queries)).reshape(rows_here, heads_here, HEAD)
    feat_key = features(keys).reshape(rows_here, heads_here, HEAD)
    value_heads = values.reshape(rows_here, heads_here, HEAD)
    before_sum = carried_in(
        scan_payload(keys, values, segment_ids), (heads_here, HEAD, HEAD), "ctx"
    )
    position = jnp.arange(rows_here)
    allowed = (position[None, :] <= position[:, None]) & (
        segment_ids[:, None] == segment_ids[None, :]
    )
    scores = jnp.einsum("thd,shd->hts", feat_query, feat_key, preferred_element_type=jnp.float32)
    weights = jnp.where(allowed[None], scores, 0.0).astype(jnp.bfloat16)
    inside = jnp.einsum("hts,she->the", weights, value_heads, preferred_element_type=jnp.float32)
    state_hi = before_sum.astype(jnp.bfloat16)
    state_lo = (before_sum - state_hi.astype(jnp.float32)).astype(jnp.bfloat16)
    carried = jnp.einsum(
        "thd,hed->the", feat_query, state_hi, preferred_element_type=jnp.float32
    ) + jnp.einsum("thd,hed->the", feat_query, state_lo, preferred_element_type=jnp.float32)
    carry_on = (segment_ids == segment_ids[0]).astype(jnp.float32)
    numerator = inside + carry_on[:, None, None] * carried
    normed = numerator * lax.rsqrt(jnp.mean(numerator * numerator, axis=-1, keepdims=True) + 1e-06)
    gain_heads = norm_gain.reshape(heads_here, HEAD)
    hidden = (normed * gain_heads[None]).astype(jnp.bfloat16).reshape(rows_here, width_here)
    return project_gathered(hidden, out_weight, "mp").astype(jnp.bfloat16)


def solution(mesh):
    in_specs = (
        P(("dp", "ctx"), "mp"),
        P(("dp", "ctx"), "mp"),
        P(("dp", "ctx"), "mp"),
        P(("dp", "ctx")),
        P("mp"),
        P(None, "mp"),
    )
    out_specs = P(("dp", "ctx"), "mp")
    return jax.shard_map(
        per_device, mesh=mesh, in_specs=in_specs, out_specs=out_specs, check_vma=False
    )
```
